256 devices in a mesh: walker: 32 (over z, x_lo, core), vec: 8 (over x_hi, y).
Axes of the slice: x: 4 (x_hi: 2, x_lo: 2; x = x_hi * 2 + x_lo), y: 4, z: 8, core: 2. Of those that a mesh axis runs over, the one named last changes fastest.
Arguments:
- copy_counts: int32 [32], P('walker'), may hold values from 0 to 2, as said below
- panels: bfloat16 [32, 200, 2048], P('walker', 'vec'), may hold values from -6 to 6
- inverse_intersection: bfloat16 [32, 200, 200], P('walker', 'vec'), may hold values from -0.4375 to 0.4375
- trial_orbitals: bfloat16 [200, 2048], replicated, may hold values from -0.0625 to 0.0625
- chol_tiles: bfloat16 [256, 128, 128], P(('walker', 'vec')), may hold values from -1.25 to 1.25
- tile_blocks: int32 [256, 2], replicated, may hold values from 0 to 15
- aux_fields: float32 [32, 64], P('walker'), may hold values from -6 to 6
Outputs:
- new_panels: bfloat16 [32, 200, 2048], P('walker', 'vec')
The draws below stay inside these ranges and needn't reach their ends.
Inputs may be any that keep to these rules, and one draw needn't show every extreme that they name: `copy_counts`: for k = 0 .. 32 let e_k be the sum of the counts of walkers 0 .. k - 1 minus k. Every e_k lies in 0 .. 1, the first and the last are 0 (the counts sum to 32), and e_k = 1 for at least one k. Some walker has exactly 2 copies.
All inputs are finite; a program needn't handle non-finite values.
Results may differ from the reference program's by a relative error of at most 0.007.
Values may be sent and summed in bfloat16 or wider, within the bound.
No kernel may reach another device: no remote copies, remote signals or barrier semaphores. Data moves between devices by JAX's collectives and lax.ppermute only.
A program may use at most 64 MiB of HBM per device.

```python
import jax
import jax.numpy as jnp
from jax import lax

M = 2048
N = 200
BS = 128
KT = 4
TERMS = 3
W_DEV = 1
NBLK = 16
TILES = 256
NVEC = 64
WALKERS = 32


def draw_copy_counts(key, part):
    device_count = WALKERS // W_DEV
    key_drift, key_spot, key_pick = jax.random.split(key, 3)
    surplus = jax.random.randint(key_drift, (device_count + 1,), 0, W_DEV + 1)
    boundary = jnp.arange(device_count + 1)
    spot = jax.random.randint(key_spot, (), 1, device_count)
    surplus = jnp.where((boundary == spot - 1) | (boundary == spot + 1), 0, surplus)
    surplus = jnp.where(boundary == spot, W_DEV, surplus)
    surplus = jnp.where((boundary == 0) | (boundary == device_count), 0, surplus)
    totals = W_DEV + surplus[1:] - surplus[:-1]
    picks = jax.random.randint(key_pick, (device_count, 2 * W_DEV), 0, W_DEV)
    row_index = jnp.arange(device_count)[:, None]
    picks = jnp.where(row_index == spot - 1, picks[:, :1], picks)
    used = jnp.arange(2 * W_DEV)[None, :] < totals[:, None]
    hits = (picks[:, :, None] == jnp.arange(W_DEV)[None, None, :]) & used[:, :, None]
    return jnp.sum(hits.astype(jnp.int32), axis=1).reshape(WALKERS).astype(jnp.int32)


def touch_ends(array, own_key, low, high):
    longest = array.shape.index(max(array.shape))
    spots = []
    for shift in (0, 1):
        where = [jax.random.randint(jax.random.fold_in(own_key, axis), (), 0, length) for axis, length in enumerate(array.shape)]
        where[longest] = (where[longest] + shift) % array.shape[longest]
        spots.append(tuple(where))
    return array.at[spots[0]].set(low).at[spots[1]].set(high)


def steps_of(rng, extent, shards, least, largest):
    def one(axis_at, blocks):
        steps = jax.random.uniform(jax.random.fold_in(jax.random.fold_in(rng, 6), axis_at), (blocks,), jnp.float32, least / len(shards), largest / len(shards))
        return jnp.repeat(jnp.exp(steps), extent[axis_at] // blocks).reshape((-1,) + (1,) * (len(extent) - axis_at - 1))

    level = one(*shards[0])
    for cut in shards[1:]:
        level = level * one(*cut)
    return level


def normal_values(own_key, shape, scale, limit, pieces=(), kind=jnp.bfloat16):
    values = jax.random.normal(own_key, shape, jnp.float32) * scale
    if len(pieces) > 0:
        values = steps_of(own_key, shape, pieces, -0.22, 0.18) * values
    return jnp.clip(values, min=-limit, max=limit).astype(kind)


def setup_inputs(seed: int = 0) -> dict:
    arg_keys = jax.random.split(jax.random.key(seed), 8)
    copy_counts = draw_copy_counts(jax.random.fold_in(arg_keys[7], 71), 0)
    panels = normal_values(arg_keys[1], (WALKERS, N, M), 1.0, 6.0, ((0, 32), (1, 8)))
    inverse_intersection = normal_values(arg_keys[2], (WALKERS, N, N), N ** -0.5, 0.4375, ((0, 32), (1, 8)))
    trial_orbitals = normal_values(arg_keys[3], (N, M), 0.012, 0.0625)
    chol_tiles = normal_values(arg_keys[4], (TILES, BS, BS), (TILES * BS // (100 * NBLK)) ** -0.5, 1.25, ((0, 256),))
    tile_blocks = touch_ends(jax.random.randint(arg_keys[5], (TILES, 2), 0, NBLK), jax.random.fold_in(arg_keys[5], 1), 0, NBLK - 1).astype(jnp.int32)
    aux_fields = normal_values(arg_keys[6], (WALKERS, NVEC), 1.0, 6.0, ((0, 32),), jnp.float32)
    return dict(copy_counts=copy_counts, panels=panels, inverse_intersection=inverse_intersection, trial_orbitals=trial_orbitals, chol_tiles=chol_tiles, tile_blocks=tile_blocks, aux_fields=aux_fields)


TIME_STEP_ROOT = 0.1


def reference(copy_counts, panels, inverse_intersection, trial_orbitals, chol_tiles, tile_blocks, aux_fields):
    running_sum = jnp.cumsum(copy_counts).astype(jnp.int32)
    new_index = jnp.arange(WALKERS, dtype=jnp.int32)
    parent = jnp.sum((running_sum[None, :] <= new_index[:, None]).astype(jnp.int32), axis=1).astype(jnp.int32)
    row_blocks = tile_blocks[:, 0].astype(jnp.int32)
    col_blocks = tile_blocks[:, 1].astype(jnp.int32)
    tiles_wide = chol_tiles.astype(jnp.float32)
    highest = lax.Precision.HIGHEST

    def walker_bias(walker_pair):
        panel_rows, inverse_rows = walker_pair
        green_rows = jnp.dot(inverse_rows, trial_orbitals, preferred_element_type=jnp.float32).astype(jnp.bfloat16)
        chosen = jnp.take(green_rows.reshape(N, NBLK, BS), col_blocks, axis=1).astype(jnp.float32)
        product = jnp.einsum('itl,tkl->itk', chosen, tiles_wide, precision=highest)
        facing = jnp.take(panel_rows.reshape(N, NBLK, BS), row_blocks, axis=1).astype(jnp.float32)
        per_tile = jnp.sum(product * facing, axis=(0, 2))
        return per_tile.reshape(NVEC, KT).sum(axis=1)

    raw_bias = lax.map(walker_bias, (panels, inverse_intersection))
    bias = jnp.clip(TIME_STEP_ROOT * raw_bias, -1.0, 1.0)
    rows_hot = (row_blocks[None, :] == jnp.arange(NBLK, dtype=jnp.int32)[:, None]).astype(jnp.float32)

    def walker_step(walker_pair):
        source, fields = walker_pair
        scales = TIME_STEP_ROOT * (fields - bias[source])
        weights = jnp.repeat(scales, KT)[None, :] * rows_hot
        series = panels[source]
        running = series.astype(jnp.float32)
        for degree in range(1, TERMS + 1):
            chosen = jnp.take(series.reshape(N, NBLK, BS), col_blocks, axis=1).astype(jnp.float32)
            product = jnp.einsum('itl,tkl->itk', chosen, tiles_wide, precision=highest)
            result = jnp.einsum('itk,at->iak', product, weights, precision=highest)
            series = (result / degree).reshape(N, M).astype(jnp.bfloat16)
            running = running + series.astype(jnp.float32)
        return running.astype(jnp.bfloat16)

    return lax.map(walker_step, (parent, aux_fields))
```

```python
import math

import jax
import jax.numpy as jnp
from jax import lax
from jax.sharding import PartitionSpec as P

KT = 4
TERMS = 3


TIME_STEP_ROOT = 0.1


def from_behind(value, axis, steps):
    count = lax.axis_size(axis)
    leading, last = (max(0, -steps), min(count, count - steps))
    return lax.ppermute(value, axis, [(source, source + steps) for source in range(leading, last)])


def tile_bias(tile_piece, row_blocks, col_blocks, panel_blocks, green_blocks):
    chosen = jnp.take(green_blocks, col_blocks, axis=2)
    product = jnp.einsum("wirl,rkl->wirk", chosen, tile_piece, preferred_element_type=jnp.float32)
    facing = jnp.take(panel_blocks, row_blocks, axis=2)
    return jnp.sum(product * facing, axis=(1, 3))


def force_bias(walker_panels, walker_inverse, trial_orbitals, chol_tiles, tile_blocks):
    walkers, cols_local, orbitals = walker_panels.shape
    tile_size = chol_tiles.shape[1]
    block_count = orbitals // tile_size
    tiles_total = tile_blocks.shape[0]
    green_rows = jnp.einsum(
        "wij,jm->wim", walker_inverse, trial_orbitals, preferred_element_type=jnp.float32
    ).astype(jnp.bfloat16)
    panel_blocks = walker_panels.reshape(walkers, cols_local, block_count, tile_size)
    green_blocks = green_rows.reshape(walkers, cols_local, block_count, tile_size)
    tile_piece = lax.all_gather(
        lax.all_gather(chol_tiles, "vec", axis=0, tiled=True), "walker", axis=0, tiled=True
    )
    contrib = tile_bias(
        tile_piece, tile_blocks[:, 0], tile_blocks[:, 1], panel_blocks, green_blocks
    )
    partial_bias = contrib
    stored = tile_piece
    partial_bias, stored = (partial_bias, stored)
    per_vector = partial_bias.reshape(walkers, tiles_total // KT, KT).sum(axis=2)
    summed_bias = lax.psum(per_vector, "vec")
    return (jnp.clip(TIME_STEP_ROOT * summed_bias, -1.0, 1.0), stored)


def propagate(start_panels, scales, stored, tile_blocks):
    slot_count, cols_local, orbitals = start_panels.shape
    tile_size = stored.shape[1]
    block_count = orbitals // tile_size
    tiles_total = stored.shape[0]
    step_tiles = math.gcd(tiles_total, 256)
    rows_hot = (
        tile_blocks[:, 0][None, :] == jnp.arange(block_count, dtype=jnp.int32)[:, None]
    ).astype(jnp.float32)
    weights = jnp.repeat(scales, KT, axis=1)[:, None, :] * rows_hot[None, :, :]
    col_blocks = tile_blocks[:, 1]
    running = start_panels.astype(jnp.float32)
    series = start_panels
    for degree in range(1, TERMS + 1):
        series_blocks = series.reshape(slot_count, cols_local, block_count, tile_size)

        def add_block(block_index, summed):
            chosen = jnp.take(series_blocks, col_blocks, axis=2)
            product = jnp.einsum(
                "qitl,tkl->qitk", chosen, stored, preferred_element_type=jnp.float32
            )
            return summed + jnp.einsum(
                "qitk,qat->qiak", product, weights, precision=lax.Precision.HIGHEST
            )

        result = lax.fori_loop(
            0,
            tiles_total // step_tiles,
            add_block,
            jnp.zeros((slot_count, cols_local, block_count, tile_size), jnp.float32),
        )
        series = (result / degree).reshape(slot_count, cols_local, orbitals).astype(jnp.bfloat16)
        running = running + series.astype(jnp.float32)
    return running.astype(jnp.bfloat16)


def shards(
    copy_counts, panels, inverse_intersection, trial_orbitals, chol_tiles, tile_blocks, aux_fields
):
    walkers = panels.shape[0]
    every_count = lax.all_gather(copy_counts, "walker", axis=0, tiled=True)
    running_sum = jnp.cumsum(every_count)
    first_slot = lax.axis_index("walker") * walkers
    bias, stored = force_bias(panels, inverse_intersection, trial_orbitals, chol_tiles, tile_blocks)
    own_sums = lax.dynamic_slice_in_dim(running_sum, first_slot, walkers, 0)
    surplus = own_sums[0] - copy_counts[0] - first_slot
    new_index = first_slot + jnp.arange(2 * walkers, dtype=jnp.int32)
    parent = jnp.minimum(
        jnp.sum((own_sums[None, :] <= new_index[:, None]).astype(jnp.int32), axis=1), walkers - 1
    )
    right_fields = from_behind(aux_fields, "walker", -1)
    field_pool = jnp.concatenate([aux_fields, right_fields], axis=0)
    scales = TIME_STEP_ROOT * (field_pool - jnp.take(bias, parent, axis=0))
    copies = propagate(jnp.take(panels, parent, axis=0), scales, stored, tile_blocks)
    arrived = from_behind(copies[walkers:], "walker", 1)
    keep_own = (jnp.arange(walkers, dtype=jnp.int32) >= surplus)[:, None, None]
    return jnp.where(keep_own, copies[:walkers], arrived)


def solution(mesh):
    return jax.shard_map(
        shards,
        mesh=mesh,
        in_specs=(
            P("walker"),
            P("walker", "vec", None),
            P("walker", "vec", None),
            P(),
            P(("walker", "vec"), None, None),
            P(),
            P("walker", None),
        ),
        out_specs=P("walker", "vec", None),
        check_vma=False,
    )
```

```python
import functools

import jax
import jax.numpy as jnp
from jax import lax
from jax.experimental import pallas as pl
from jax.experimental.pallas import tpu as pltpu
from jax.sharding import PartitionSpec as P

KT = 4
TERMS = 3
TIME_STEP_ROOT = 0.1
ROWS = 32
INTERPRET = False


def shift_from(value, axis, steps):
    count = lax.axis_size(axis)
    return lax.ppermute(value, axis, [(i, i + steps) for i in range(count - steps)])


def butterfly_sum(value, axis):
    count = lax.axis_size(axis)
    step = 1
    while step < count:
        value = value + lax.ppermute(value, axis, [(i, i ^ step) for i in range(count)])
        step *= 2
    return value


def bias_kernel(rb_ref, cb_ref, pt_ref, g_ref, tiles_ref, out_ref, m_ref):
    blocks, size, _ = m_ref.shape
    for a in range(blocks):
        m_ref[a] = jnp.dot(
            pt_ref[a * size:(a + 1) * size, :], g_ref[...], preferred_element_type=jnp.float32
        )

    def one(t, carry):
        col = pl.multiple_of(cb_ref[t] * size, size)
        blk = m_ref[rb_ref[t], :, pl.ds(col, size)]
        prod = blk * tiles_ref[t].astype(jnp.float32)
        out_ref[pl.ds(t, 1), :] = jnp.sum(prod, axis=0, keepdims=True)
        return carry

    lax.fori_loop(0, tiles_ref.shape[0], one, 0)


def tile_bias(panel_t, green, tiles, rb, cb):
    tiles_total, size, _ = tiles.shape
    orbitals = green.shape[1]
    blocks = orbitals // size
    return pl.pallas_call(
        bias_kernel,
        out_shape=jax.ShapeDtypeStruct((tiles_total, size), jnp.float32),
        in_specs=[
            pl.BlockSpec(memory_space=pltpu.SMEM),
            pl.BlockSpec(memory_space=pltpu.SMEM),
            pl.BlockSpec(memory_space=pltpu.VMEM),
            pl.BlockSpec(memory_space=pltpu.VMEM),
            pl.BlockSpec(memory_space=pltpu.VMEM),
        ],
        out_specs=pl.BlockSpec(memory_space=pltpu.VMEM),
        scratch_shapes=[pltpu.VMEM((blocks, size, orbitals), jnp.float32)],
        compiler_params=pltpu.CompilerParams(vmem_limit_bytes=48 * 1024 * 1024),
        interpret=INTERPRET,
    )(rb, cb, panel_t, green, tiles)


def prop_kernel(rb_ref, cb_ref, s_ref, x_ref, tiles_ref, out_ref, a_ref, hi_ref, lo_ref, y_ref):
    blocks, size, orbitals = a_ref.shape
    a_ref[...] = jnp.zeros(a_ref.shape, jnp.float32)

    def build(t, carry):
        col = pl.multiple_of(cb_ref[t] * size, size)
        row = rb_ref[t]
        a_ref[row, :, pl.ds(col, size)] += s_ref[t] * tiles_ref[t].astype(jnp.float32)
        return carry

    lax.fori_loop(0, tiles_ref.shape[0], build, 0)

    def split(a, carry):
        whole = a_ref[a]
        high = whole.astype(jnp.bfloat16)
        hi_ref[a] = high
        lo_ref[a] = (whole - high.astype(jnp.float32)).astype(jnp.bfloat16)
        return carry

    lax.fori_loop(0, blocks, split, 0)

    dims = (((1,), (1,)), ((), ()))
    series = x_ref[...]
    running = series.astype(jnp.float32)
    for degree in range(1, TERMS + 1):
        for a in range(blocks):
            y_ref[:, a * size:(a + 1) * size] = lax.dot_general(
                series, hi_ref[a], dims, preferred_element_type=jnp.float32
            ) + lax.dot_general(series, lo_ref[a], dims, preferred_element_type=jnp.float32)
        series = (y_ref[...] / degree).astype(jnp.bfloat16)
        running = running + series.astype(jnp.float32)
    out_ref[...] = running.astype(out_ref.dtype)


def propagate(x0, tiles, rb, cb, scales):
    tiles_total, size, _ = tiles.shape
    rows, orbitals = x0.shape
    blocks = orbitals // size
    return pl.pallas_call(
        prop_kernel,
        out_shape=jax.ShapeDtypeStruct((rows, orbitals), jnp.bfloat16),
        in_specs=[
            pl.BlockSpec(memory_space=pltpu.SMEM),
            pl.BlockSpec(memory_space=pltpu.SMEM),
            pl.BlockSpec(memory_space=pltpu.SMEM),
            pl.BlockSpec(memory_space=pltpu.VMEM),
            pl.BlockSpec(memory_space=pltpu.VMEM),
        ],
        out_specs=pl.BlockSpec(memory_space=pltpu.VMEM),
        scratch_shapes=[
            pltpu.VMEM((blocks, size, orbitals), jnp.float32),
            pltpu.VMEM((blocks, size, orbitals), jnp.bfloat16),
            pltpu.VMEM((blocks, size, orbitals), jnp.bfloat16),
            pltpu.VMEM((rows, orbitals), jnp.float32),
        ],
        compiler_params=pltpu.CompilerParams(vmem_limit_bytes=56 * 1024 * 1024),
        interpret=INTERPRET,
    )(rb, cb, scales, x0, tiles)


def pad_rows(x):
    return jnp.pad(x, ((0, ROWS - x.shape[0]), (0, 0)))


def shards(
    copy_counts, panels, inverse_intersection, trial_orbitals, chol_tiles, tile_blocks, aux_fields
):
    cols_local = panels.shape[1]
    walker_id = lax.axis_index("walker")
    running = copy_counts
    step = 1
    while step < lax.axis_size("walker"):
        running = running + shift_from(running, "walker", step)
        step *= 2
    surplus = running[0] - copy_counts[0] - walker_id
    from_prev = surplus > 0

    prev_panel = shift_from(panels, "walker", 1)
    tiles = lax.all_gather(
        lax.all_gather(chol_tiles, "vec", axis=0, tiled=True), "walker", axis=0, tiled=True
    )
    rb = tile_blocks[:, 0]
    cb = tile_blocks[:, 1]
    tiles_total = tiles.shape[0]

    own = panels[0]
    green = jnp.dot(
        inverse_intersection[0], trial_orbitals, preferred_element_type=jnp.float32
    ).astype(jnp.bfloat16)
    partial = tile_bias(pad_rows(own).T, pad_rows(green), tiles, rb, cb)
    per_vector = partial.reshape(tiles_total // KT, KT * partial.shape[1]).sum(axis=1)
    raw = butterfly_sum(per_vector, "vec")
    bias_own = jnp.clip(TIME_STEP_ROOT * raw, -1.0, 1.0)
    bias_prev = shift_from(bias_own, "walker", 1)
    bias = jnp.where(from_prev, bias_prev, bias_own)
    scales = TIME_STEP_ROOT * (aux_fields[0] - bias)
    tile_scales = jnp.repeat(scales, KT)
    start = jnp.where(from_prev, prev_panel[0], own)
    out = propagate(pad_rows(start), tiles, rb, cb, tile_scales)
    return out[:cols_local][None]


def solution(mesh):
    return jax.shard_map(
        shards,
        mesh=mesh,
        in_specs=(
            P("walker"),
            P("walker", "vec", None),
            P("walker", "vec", None),
            P(),
            P(("walker", "vec"), None, None),
            P(),
            P("walker", None),
        ),
        out_specs=P("walker", "vec", None),
        check_vma=False,
    )
```

```python
import functools

import jax
import jax.numpy as jnp
from jax import lax
from jax.experimental import pallas as pl
from jax.experimental.pallas import tpu as pltpu
from jax.sharding import PartitionSpec as P

KT = 4
TERMS = 3
TIME_STEP_ROOT = 0.1
ROWS = 32
INTERPRET = False


def shift_from(value, axis, steps):
    count = lax.axis_size(axis)
    return lax.ppermute(value, axis, [(i, i + steps) for i in range(count - steps)])


def butterfly_sum(value, axis):
    count = lax.axis_size(axis)
    step = 1
    while step < count:
        value = value + lax.ppermute(value, axis, [(i, i ^ step) for i in range(count)])
        step *= 2
    return value


def bias_kernel(*refs):
    count = len(STREAMS)
    rbs, cbs = refs[:count], refs[count:2 * count]
    pt_ref, g_ref = refs[2 * count], refs[2 * count + 1]
    parts = refs[2 * count + 2:3 * count + 2]
    outs = refs[3 * count + 2:4 * count + 2]
    m_ref = refs[-1]
    blocks, size, _ = m_ref.shape
    for a in range(blocks):
        m_ref[a] = jnp.dot(
            pt_ref[a * size:(a + 1) * size, :], g_ref[...], preferred_element_type=jnp.float32
        )
    for (_, low, high), rb_ref, cb_ref, part_ref, out_ref in zip(STREAMS, rbs, cbs, parts, outs):

        def one(t, carry, rb_ref=rb_ref, cb_ref=cb_ref, part_ref=part_ref, out_ref=out_ref, low=low, high=high):
            col = pl.multiple_of(cb_ref[t] * size, size)
            blk = m_ref[rb_ref[t], low:high, pl.ds(col, size)]
            prod = blk * part_ref[t].astype(jnp.float32)
            out_ref[pl.ds(t, 1), :] = jnp.sum(prod, axis=0, keepdims=True)
            return carry

        lax.fori_loop(0, part_ref.shape[0], one, 0)


def tile_bias(panel_t, green, parts, rbs, cbs):
    tiles_total, _, size = parts[0].shape
    orbitals = green.shape[1]
    blocks = orbitals // size
    count = len(parts)
    smem = pl.BlockSpec(memory_space=pltpu.SMEM)
    vmem = pl.BlockSpec(memory_space=pltpu.VMEM)
    return pl.pallas_call(
        bias_kernel,
        out_shape=[jax.ShapeDtypeStruct((tiles_total, size), jnp.float32)] * count,
        in_specs=[smem] * (2 * count) + [vmem] * (2 + count),
        out_specs=[vmem] * count,
        scratch_shapes=[pltpu.VMEM((blocks, size, orbitals), jnp.float32)],
        compiler_params=pltpu.CompilerParams(vmem_limit_bytes=48 * 1024 * 1024),
        interpret=INTERPRET,
    )(*rbs, *cbs, panel_t, green, *parts)


def prop_kernel(*refs):
    count = len(STREAMS)
    rbs, cbs, ss = refs[:count], refs[count:2 * count], refs[2 * count:3 * count]
    x_ref = refs[3 * count]
    parts = refs[3 * count + 1:4 * count + 1]
    out_ref, a_ref, hi_ref, lo_ref, y_ref = refs[4 * count + 1:]
    blocks, size, orbitals = a_ref.shape
    a_ref[...] = jnp.zeros(a_ref.shape, jnp.float32)
    for (_, low, high), rb_ref, cb_ref, s_ref, part_ref in zip(STREAMS, rbs, cbs, ss, parts):

        def build(t, carry, rb_ref=rb_ref, cb_ref=cb_ref, s_ref=s_ref, part_ref=part_ref, low=low, high=high):
            col = pl.multiple_of(cb_ref[t] * size, size)
            row = rb_ref[t]
            a_ref[row, low:high, pl.ds(col, size)] += s_ref[t] * part_ref[t].astype(jnp.float32)
            return carry

        lax.fori_loop(0, part_ref.shape[0], build, 0)

    def split(a, carry):
        whole = a_ref[a]
        high = whole.astype(jnp.bfloat16)
        hi_ref[a] = high
        lo_ref[a] = (whole - high.astype(jnp.float32)).astype(jnp.bfloat16)
        return carry

    lax.fori_loop(0, blocks, split, 0)

    dims = (((1,), (1,)), ((), ()))
    series = x_ref[...]
    running = series.astype(jnp.float32)
    for degree in range(1, TERMS + 1):
        for a in range(blocks):
            y_ref[:, a * size:(a + 1) * size] = lax.dot_general(
                series, hi_ref[a], dims, preferred_element_type=jnp.float32
            ) + lax.dot_general(series, lo_ref[a], dims, preferred_element_type=jnp.float32)
        series = (y_ref[...] / degree).astype(jnp.bfloat16)
        running = running + series.astype(jnp.float32)
    out_ref[...] = running.astype(out_ref.dtype)


def propagate(x0, parts, rbs, cbs, ss):
    size = parts[0].shape[2]
    rows, orbitals = x0.shape
    blocks = orbitals // size
    count = len(parts)
    smem = pl.BlockSpec(memory_space=pltpu.SMEM)
    vmem = pl.BlockSpec(memory_space=pltpu.VMEM)
    return pl.pallas_call(
        prop_kernel,
        out_shape=jax.ShapeDtypeStruct((rows, orbitals), jnp.bfloat16),
        in_specs=[smem] * (3 * count) + [vmem] * (1 + count),
        out_specs=vmem,
        scratch_shapes=[
            pltpu.VMEM((blocks, size, orbitals), jnp.float32),
            pltpu.VMEM((blocks, size, orbitals), jnp.bfloat16),
            pltpu.VMEM((blocks, size, orbitals), jnp.bfloat16),
            pltpu.VMEM((rows, orbitals), jnp.float32),
        ],
        compiler_params=pltpu.CompilerParams(vmem_limit_bytes=56 * 1024 * 1024),
        interpret=INTERPRET,
    )(*rbs, *cbs, *ss, x0, *parts)


STREAMS = (
    ((("walker", 16), ("walker", 8), ("walker", 4), ("vec", 4), ("walker", 2), ("vec", 2), ("vec", 1), ("walker", 1)), 0, 48),
    ((("vec", 2), ("vec", 1), ("walker", 16), ("walker", 8), ("walker", 4), ("vec", 4), ("walker", 2), ("walker", 1)), 48, 96),
    ((("vec", 4), ("walker", 2), ("vec", 2), ("vec", 1), ("walker", 16), ("walker", 8), ("walker", 4), ("walker", 1)), 96, 128),
)


def xor_gather(x, order):
    for axis, step in order:
        count = lax.axis_size(axis)
        other = lax.ppermute(x, axis, [(i, i ^ step) for i in range(count)])
        x = jnp.concatenate([x, other], axis=0)
    return x


def source_tiles(order):
    position = jnp.arange(2 ** len(order), dtype=jnp.int32)
    masks = {"walker": jnp.zeros_like(position), "vec": jnp.zeros_like(position)}
    for bit, (axis, step) in enumerate(order):
        masks[axis] = masks[axis] + ((position >> bit) & 1) * step
    walker = jnp.bitwise_xor(lax.axis_index("walker"), masks["walker"])
    vec = jnp.bitwise_xor(lax.axis_index("vec"), masks["vec"])
    return walker * lax.axis_size("vec") + vec


def pad_rows(x):
    return jnp.pad(x, ((0, ROWS - x.shape[0]), (0, 0)))


def shards(
    copy_counts, panels, inverse_intersection, trial_orbitals, chol_tiles, tile_blocks, aux_fields
):
    cols_local = panels.shape[1]
    walker_id = lax.axis_index("walker")
    running = copy_counts
    step = 1
    while step < lax.axis_size("walker"):
        running = running + shift_from(running, "walker", step)
        step *= 2
    from_prev = running[0] - copy_counts[0] - walker_id > 0

    prev_panel = shift_from(panels, "walker", 1)
    prev_inverse = shift_from(inverse_intersection, "walker", 1)
    parts, rbs, cbs, sources = [], [], [], []
    for order, low, high in STREAMS:
        parts.append(xor_gather(chol_tiles[:, low:high], order))
        source = source_tiles(order)
        sources.append(source)
        rbs.append(jnp.take(tile_blocks[:, 0], source))
        cbs.append(jnp.take(tile_blocks[:, 1], source))

    start = jnp.where(from_prev, prev_panel[0], panels[0])
    inverse = jnp.where(from_prev, prev_inverse[0], inverse_intersection[0])
    green = jnp.dot(inverse, trial_orbitals, preferred_element_type=jnp.float32).astype(jnp.bfloat16)
    partials = tile_bias(pad_rows(start).T, pad_rows(green), parts, rbs, cbs)
    vectors = tile_blocks.shape[0] // KT
    ids = jnp.concatenate([source // KT for source in sources])
    values = jnp.concatenate([partial.sum(axis=1) for partial in partials])
    hot = ids[:, None] == jnp.arange(vectors, dtype=ids.dtype)[None, :]
    per_vector = jnp.sum(jnp.where(hot, values[:, None], 0.0), axis=0)
    raw = butterfly_sum(per_vector, "vec")
    bias = jnp.clip(TIME_STEP_ROOT * raw, -1.0, 1.0)
    scales = TIME_STEP_ROOT * (aux_fields[0] - bias)
    ss = [jnp.take(scales, source // KT) for source in sources]
    out = propagate(pad_rows(start), parts, rbs, cbs, ss)
    return out[:cols_local][None]


def solution(mesh):
    return jax.shard_map(
        shards,
        mesh=mesh,
        in_specs=(
            P("walker"),
            P("walker", "vec", None),
            P("walker", "vec", None),
            P(),
            P(("walker", "vec"), None, None),
            P(),
            P("walker", None),
        ),
        out_specs=P("walker", "vec", None),
        check_vma=False,
    )
```

```python
import functools

import jax
import jax.numpy as jnp
from jax import lax
from jax.experimental import pallas as pl
from jax.experimental.pallas import tpu as pltpu
from jax.sharding import PartitionSpec as P

KT = 4
TERMS = 3
TIME_STEP_ROOT = 0.1
ROWS = 32
INTERPRET = False


def shift_from(value, axis, steps):
    count = lax.axis_size(axis)
    return lax.ppermute(value, axis, [(i, i + steps) for i in range(count - steps)])


def butterfly_sum(value, axis):
    count = lax.axis_size(axis)
    step = 1
    while step < count:
        value = value + lax.ppermute(value, axis, [(i, i ^ step) for i in range(count)])
        step *= 2
    return value


def bias_kernel(*refs):
    count = len(STREAMS)
    rbs, cbs = refs[:count], refs[count:2 * count]
    pt_ref, g_ref = refs[2 * count], refs[2 * count + 1]
    parts = refs[2 * count + 2:3 * count + 2]
    outs = refs[3 * count + 2:4 * count + 2]
    m_ref = refs[-1]
    blocks, size, _ = m_ref.shape
    for a in range(blocks):
        m_ref[a] = jnp.dot(
            pt_ref[a * size:(a + 1) * size, :], g_ref[...], preferred_element_type=jnp.float32
        )
    for (_, low, high), rb_ref, cb_ref, part_ref, out_ref in zip(STREAMS, rbs, cbs, parts, outs):

        def one(t, carry, rb_ref=rb_ref, cb_ref=cb_ref, part_ref=part_ref, out_ref=out_ref, low=low, high=high):
            col = pl.multiple_of(cb_ref[t] * size, size)
            blk = m_ref[rb_ref[t], low:high, pl.ds(col, size)]
            prod = blk * part_ref[t, 0:high - low, :].astype(jnp.float32)
            out_ref[pl.ds(t, 1), :] = jnp.sum(prod, axis=0, keepdims=True)
            return carry

        lax.fori_loop(0, part_ref.shape[0], one, 0)


def tile_bias(panel_t, green, parts, rbs, cbs):
    tiles_total, _, size = parts[0].shape
    orbitals = green.shape[1]
    blocks = orbitals // size
    count = len(parts)
    smem = pl.BlockSpec(memory_space=pltpu.SMEM)
    vmem = pl.BlockSpec(memory_space=pltpu.VMEM)
    return pl.pallas_call(
        bias_kernel,
        out_shape=[jax.ShapeDtypeStruct((tiles_total, size), jnp.float32)] * count,
        in_specs=[smem] * (2 * count) + [vmem] * (2 + count),
        out_specs=[vmem] * count,
        scratch_shapes=[pltpu.VMEM((blocks, size, orbitals), jnp.float32)],
        compiler_params=pltpu.CompilerParams(vmem_limit_bytes=48 * 1024 * 1024),
        interpret=INTERPRET,
    )(*rbs, *cbs, panel_t, green, *parts)


def prop_kernel(*refs):
    count = len(STREAMS)
    rbs, cbs, ss = refs[:count], refs[count:2 * count], refs[2 * count:3 * count]
    x_ref = refs[3 * count]
    parts = refs[3 * count + 1:4 * count + 1]
    out_ref, a_ref, hi_ref, lo_ref, y_ref = refs[4 * count + 1:]
    blocks, size, orbitals = a_ref.shape
    a_ref[...] = jnp.zeros(a_ref.shape, jnp.float32)
    for (_, low, high), rb_ref, cb_ref, s_ref, part_ref in zip(STREAMS, rbs, cbs, ss, parts):

        def build(t, carry, rb_ref=rb_ref, cb_ref=cb_ref, s_ref=s_ref, part_ref=part_ref, low=low, high=high):
            col = pl.multiple_of(cb_ref[t] * size, size)
            row = rb_ref[t]
            a_ref[row, low:high, pl.ds(col, size)] += s_ref[t] * part_ref[t, 0:high - low, :].astype(jnp.float32)
            return carry

        lax.fori_loop(0, part_ref.shape[0], build, 0)

    def split(a, carry):
        whole = a_ref[a]
        high = whole.astype(jnp.bfloat16)
        hi_ref[a] = high
        lo_ref[a] = (whole - high.astype(jnp.float32)).astype(jnp.bfloat16)
        return carry

    lax.fori_loop(0, blocks, split, 0)

    dims = (((1,), (1,)), ((), ()))
    series = x_ref[...]
    running = series.astype(jnp.float32)
    for degree in range(1, TERMS + 1):
        for a in range(blocks):
            y_ref[:, a * size:(a + 1) * size] = lax.dot_general(
                series, hi_ref[a], dims, preferred_element_type=jnp.float32
            ) + lax.dot_general(series, lo_ref[a], dims, preferred_element_type=jnp.float32)
        series = (y_ref[...] / degree).astype(jnp.bfloat16)
        running = running + series.astype(jnp.float32)
    out_ref[...] = running.astype(out_ref.dtype)


def propagate(x0, parts, rbs, cbs, ss):
    size = parts[0].shape[2]
    rows, orbitals = x0.shape
    blocks = orbitals // size
    count = len(parts)
    smem = pl.BlockSpec(memory_space=pltpu.SMEM)
    vmem = pl.BlockSpec(memory_space=pltpu.VMEM)
    return pl.pallas_call(
        prop_kernel,
        out_shape=jax.ShapeDtypeStruct((rows, orbitals), jnp.bfloat16),
        in_specs=[smem] * (3 * count) + [vmem] * (1 + count),
        out_specs=vmem,
        scratch_shapes=[
            pltpu.VMEM((blocks, size, orbitals), jnp.float32),
            pltpu.VMEM((blocks, size, orbitals), jnp.bfloat16),
            pltpu.VMEM((blocks, size, orbitals), jnp.bfloat16),
            pltpu.VMEM((rows, orbitals), jnp.float32),
        ],
        compiler_params=pltpu.CompilerParams(vmem_limit_bytes=56 * 1024 * 1024),
        interpret=INTERPRET,
    )(*rbs, *cbs, *ss, x0, *parts)


STREAMS = (
    ((("walker", 16), ("walker", 8), ("walker", 4), ("vec", 4), ("walker", 2), ("vec", 2), ("vec", 1), ("walker", 1)), 0, 48),
    ((("vec", 2), ("vec", 1), ("walker", 16), ("walker", 8), ("walker", 4), ("vec", 4), ("walker", 2), ("walker", 1)), 48, 96),
    ((("vec", 4), ("walker", 2), ("vec", 2), ("vec", 1), ("walker", 16), ("walker", 8), ("walker", 4), ("walker", 1)), 96, 128),
)


def xor_gather(x, order):
    for axis, step in order:
        count = lax.axis_size(axis)
        other = lax.ppermute(x, axis, [(i, i ^ step) for i in range(count)])
        x = jnp.concatenate([x, other], axis=0)
    return x


def source_tiles(order):
    position = jnp.arange(2 ** len(order), dtype=jnp.int32)
    masks = {"walker": jnp.zeros_like(position), "vec": jnp.zeros_like(position)}
    for bit, (axis, step) in enumerate(order):
        masks[axis] = masks[axis] + ((position >> bit) & 1) * step
    walker = jnp.bitwise_xor(lax.axis_index("walker"), masks["walker"])
    vec = jnp.bitwise_xor(lax.axis_index("vec"), masks["vec"])
    return walker * lax.axis_size("vec") + vec


def pick(table, index):
    hot = index[:, None] == jnp.arange(table.shape[0], dtype=index.dtype)[None, :]
    return jnp.sum(jnp.where(hot, table[None, :], jnp.zeros((), table.dtype)), axis=1)


def pad_rows(x):
    return jnp.pad(x, ((0, ROWS - x.shape[0]), (0, 0)))


def shards(
    copy_counts, panels, inverse_intersection, trial_orbitals, chol_tiles, tile_blocks, aux_fields
):
    cols_local = panels.shape[1]
    walker_id = lax.axis_index("walker")
    vec_id = lax.axis_index("vec")
    vecs = lax.axis_size("vec")
    prev_panel = shift_from(panels, "walker", 1)
    prev_inverse = shift_from(inverse_intersection, "walker", 1)
    size = chol_tiles.shape[2]
    meta = jnp.zeros((1, 16, size), chol_tiles.dtype).at[0, 0, 0].set(copy_counts[0].astype(chol_tiles.dtype))
    parts, rbs, cbs, sources = [], [], [], []
    for index, (order, low, high) in enumerate(STREAMS):
        piece = chol_tiles[:, low:high]
        if index == len(STREAMS) - 1:
            piece = jnp.concatenate([piece, meta], axis=1)
        parts.append(xor_gather(piece, order))
        source = source_tiles(order)
        sources.append(source)
        rbs.append(pick(tile_blocks[:, 0], source))
        cbs.append(pick(tile_blocks[:, 1], source))
    last = STREAMS[-1]
    counts = parts[-1][:, last[2] - last[1], 0].astype(jnp.float32)
    source = sources[-1]
    before = (source % vecs == vec_id) & (source // vecs < walker_id)
    surplus = jnp.sum(jnp.where(before, counts, 0.0)) - walker_id.astype(jnp.float32)
    from_prev = surplus > 0.5

    green_own = jnp.dot(inverse_intersection[0], trial_orbitals, preferred_element_type=jnp.float32).astype(jnp.bfloat16)
    green_prev = jnp.dot(prev_inverse[0], trial_orbitals, preferred_element_type=jnp.float32).astype(jnp.bfloat16)
    start = jnp.where(from_prev, prev_panel[0], panels[0])
    green = jnp.where(from_prev, green_prev, green_own)
    partials = tile_bias(pad_rows(start).T, pad_rows(green), parts, rbs, cbs)
    vectors = tile_blocks.shape[0] // KT
    ids = jnp.concatenate([source // KT for source in sources])
    values = jnp.concatenate([partial.sum(axis=1) for partial in partials])
    hot = ids[:, None] == jnp.arange(vectors, dtype=ids.dtype)[None, :]
    per_vector = jnp.sum(jnp.where(hot, values[:, None], 0.0), axis=0)
    raw = butterfly_sum(per_vector, "vec")
    bias = jnp.clip(TIME_STEP_ROOT * raw, -1.0, 1.0)
    scales = TIME_STEP_ROOT * (aux_fields[0] - bias)
    ss = [pick(scales, source // KT) for source in sources]
    out = propagate(pad_rows(start), parts, rbs, cbs, ss)
    return out[:cols_local][None]


def solution(mesh):
    return jax.shard_map(
        shards,
        mesh=mesh,
        in_specs=(
            P("walker"),
            P("walker", "vec", None),
            P("walker", "vec", None),
            P(),
            P(("walker", "vec"), None, None),
            P(),
            P("walker", None),
        ),
        out_specs=P("walker", "vec", None),
        check_vma=False,
    )
```

```python
import functools

import jax
import jax.numpy as jnp
from jax import lax
from jax.experimental import pallas as pl
from jax.experimental.pallas import tpu as pltpu
from jax.sharding import PartitionSpec as P

KT = 4
TERMS = 3
TIME_STEP_ROOT = 0.1
ROWS = 32
INTERPRET = False


def shift_from(value, axis, steps):
    count = lax.axis_size(axis)
    return lax.ppermute(value, axis, [(i, i + steps) for i in range(count - steps)])


def butterfly_sum(value, axis):
    count = lax.axis_size(axis)
    step = 1
    while step < count:
        value = value + lax.ppermute(value, axis, [(i, i ^ step) for i in range(count)])
        step *= 2
    return value


def bias_kernel(*refs):
    count = len(STREAMS)
    rbs, cbs = refs[:count], refs[count:2 * count]
    pt_ref, g_ref = refs[2 * count], refs[2 * count + 1]
    parts = refs[2 * count + 2:3 * count + 2]
    outs = refs[3 * count + 2:4 * count + 2]
    m_ref = refs[-1]
    blocks, size, _ = m_ref.shape
    for a in range(blocks):
        m_ref[a] = jnp.dot(
            pt_ref[a * size:(a + 1) * size, :], g_ref[...], preferred_element_type=jnp.float32
        )

    def one(t, carry):
        for (_, low, high), rb_ref, cb_ref, part_ref, out_ref in zip(STREAMS, rbs, cbs, parts, outs):
            col = pl.multiple_of(cb_ref[t] * size, size)
            blk = m_ref[rb_ref[t], low:high, pl.ds(col, size)]
            prod = blk * part_ref[t, 0:high - low, :].astype(jnp.float32)
            out_ref[pl.ds(t, 1), :] = jnp.sum(prod, axis=0, keepdims=True)
        return carry

    lax.fori_loop(0, parts[0].shape[0], one, 0, unroll=2)


def tile_bias(panel_t, green, parts, rbs, cbs):
    tiles_total, _, size = parts[0].shape
    orbitals = green.shape[1]
    blocks = orbitals // size
    count = len(parts)
    smem = pl.BlockSpec(memory_space=pltpu.SMEM)
    vmem = pl.BlockSpec(memory_space=pltpu.VMEM)
    return pl.pallas_call(
        bias_kernel,
        out_shape=[jax.ShapeDtypeStruct((tiles_total, size), jnp.float32)] * count,
        in_specs=[smem] * (2 * count) + [vmem] * (2 + count),
        out_specs=[vmem] * count,
        scratch_shapes=[pltpu.VMEM((blocks, size, orbitals), jnp.float32)],
        compiler_params=pltpu.CompilerParams(vmem_limit_bytes=48 * 1024 * 1024),
        interpret=INTERPRET,
    )(*rbs, *cbs, panel_t, green, *parts)


def prop_kernel(*refs):
    count = len(STREAMS)
    rbs, cbs, ss = refs[:count], refs[count:2 * count], refs[2 * count:3 * count]
    x_ref = refs[3 * count]
    parts = refs[3 * count + 1:4 * count + 1]
    out_ref, hi_ref, lo_ref, y_ref = refs[4 * count + 1:]
    orbitals = hi_ref.shape[0]
    size = parts[0].shape[2]
    hi_ref[...] = jnp.zeros(hi_ref.shape, hi_ref.dtype)
    lo_ref[...] = jnp.zeros(lo_ref.shape, lo_ref.dtype)

    def build(t, carry):
        for (_, low, high), rb_ref, cb_ref, s_ref, part_ref in zip(STREAMS, rbs, cbs, ss, parts):
            rows = pl.ds(pl.multiple_of(rb_ref[t] * size + low, 16), high - low)
            cols = pl.ds(pl.multiple_of(cb_ref[t] * size, size), size)
            whole = (
                hi_ref[rows, cols].astype(jnp.float32)
                + lo_ref[rows, cols].astype(jnp.float32)
                + s_ref[t] * part_ref[t, 0:high - low, :].astype(jnp.float32)
            )
            upper = whole.astype(jnp.bfloat16)
            hi_ref[rows, cols] = upper
            lo_ref[rows, cols] = (whole - upper.astype(jnp.float32)).astype(jnp.bfloat16)
        return carry

    lax.fori_loop(0, parts[0].shape[0], build, 0)

    dims = (((1,), (1,)), ((), ()))
    chunk = 512
    series = x_ref[...]
    running = series.astype(jnp.float32)
    for degree in range(1, TERMS + 1):
        for c in range(orbitals // chunk):
            span = slice(c * chunk, (c + 1) * chunk)
            y_ref[:, span] = lax.dot_general(
                series, hi_ref[span, :], dims, preferred_element_type=jnp.float32
            ) + lax.dot_general(series, lo_ref[span, :], dims, preferred_element_type=jnp.float32)
        series = (y_ref[...] / degree).astype(jnp.bfloat16)
        running = running + series.astype(jnp.float32)
    out_ref[...] = running.astype(out_ref.dtype)


def propagate(x0, parts, rbs, cbs, ss):
    size = parts[0].shape[2]
    rows, orbitals = x0.shape
    blocks = orbitals // size
    count = len(parts)
    smem = pl.BlockSpec(memory_space=pltpu.SMEM)
    vmem = pl.BlockSpec(memory_space=pltpu.VMEM)
    return pl.pallas_call(
        prop_kernel,
        out_shape=jax.ShapeDtypeStruct((rows, orbitals), jnp.bfloat16),
        in_specs=[smem] * (3 * count) + [vmem] * (1 + count),
        out_specs=vmem,
        scratch_shapes=[
            pltpu.VMEM((orbitals, orbitals), jnp.bfloat16),
            pltpu.VMEM((orbitals, orbitals), jnp.bfloat16),
            pltpu.VMEM((rows, orbitals), jnp.float32),
        ],
        compiler_params=pltpu.CompilerParams(vmem_limit_bytes=48 * 1024 * 1024),
        interpret=INTERPRET,
    )(*rbs, *cbs, *ss, x0, *parts)


STREAMS = (
    ((("walker", 16), ("walker", 8), ("walker", 4), ("vec", 4), ("walker", 2), ("vec", 2), ("vec", 1), ("walker", 1)), 0, 48),
    ((("vec", 2), ("vec", 1), ("walker", 16), ("walker", 8), ("walker", 4), ("vec", 4), ("walker", 2), ("walker", 1)), 48, 96),
    ((("vec", 4), ("walker", 2), ("vec", 2), ("vec", 1), ("walker", 16), ("walker", 8), ("walker", 4), ("walker", 1)), 96, 128),
)


def xor_gather(x, order):
    for axis, step in order:
        count = lax.axis_size(axis)
        other = lax.ppermute(x, axis, [(i, i ^ step) for i in range(count)])
        x = jnp.concatenate([x, other], axis=0)
    return x


def source_tiles(order):
    position = jnp.arange(2 ** len(order), dtype=jnp.int32)
    masks = {"walker": jnp.zeros_like(position), "vec": jnp.zeros_like(position)}
    for bit, (axis, step) in enumerate(order):
        masks[axis] = masks[axis] + ((position >> bit) & 1) * step
    walker = jnp.bitwise_xor(lax.axis_index("walker"), masks["walker"])
    vec = jnp.bitwise_xor(lax.axis_index("vec"), masks["vec"])
    return walker * lax.axis_size("vec") + vec


def pick(table, index):
    hot = index[:, None] == jnp.arange(table.shape[0], dtype=index.dtype)[None, :]
    return jnp.sum(jnp.where(hot, table[None, :], jnp.zeros((), table.dtype)), axis=1)


def pad_rows(x):
    return jnp.pad(x, ((0, ROWS - x.shape[0]), (0, 0)))


def shards(
    copy_counts, panels, inverse_intersection, trial_orbitals, chol_tiles, tile_blocks, aux_fields
):
    cols_local = panels.shape[1]
    walker_id = lax.axis_index("walker")
    vec_id = lax.axis_index("vec")
    vecs = lax.axis_size("vec")
    prev_panel = shift_from(panels, "walker", 1)
    prev_inverse = shift_from(inverse_intersection, "walker", 1)
    size = chol_tiles.shape[2]
    meta = jnp.zeros((1, 16, size), chol_tiles.dtype).at[0, 0, 0].set(copy_counts[0].astype(chol_tiles.dtype))
    parts, rbs, cbs, sources = [], [], [], []
    for index, (order, low, high) in enumerate(STREAMS):
        piece = chol_tiles[:, low:high]
        if index == len(STREAMS) - 1:
            piece = jnp.concatenate([piece, meta], axis=1)
        parts.append(xor_gather(piece, order))
        source = source_tiles(order)
        sources.append(source)
        rbs.append(pick(tile_blocks[:, 0], source))
        cbs.append(pick(tile_blocks[:, 1], source))
    last = STREAMS[-1]
    counts = parts[-1][:, last[2] - last[1], 0].astype(jnp.float32)
    source = sources[-1]
    before = (source % vecs == vec_id) & (source // vecs < walker_id)
    surplus = jnp.sum(jnp.where(before, counts, 0.0)) - walker_id.astype(jnp.float32)
    from_prev = surplus > 0.5

    green_own = jnp.dot(inverse_intersection[0], trial_orbitals, preferred_element_type=jnp.float32).astype(jnp.bfloat16)
    green_prev = jnp.dot(prev_inverse[0], trial_orbitals, preferred_element_type=jnp.float32).astype(jnp.bfloat16)
    start = jnp.where(from_prev, prev_panel[0], panels[0])
    green = jnp.where(from_prev, green_prev, green_own)
    partials = tile_bias(pad_rows(start).T, pad_rows(green), parts, rbs, cbs)
    vectors = tile_blocks.shape[0] // KT
    ids = jnp.concatenate([source // KT for source in sources])
    values = jnp.concatenate([partial.sum(axis=1) for partial in partials])
    hot = ids[:, None] == jnp.arange(vectors, dtype=ids.dtype)[None, :]
    per_vector = jnp.sum(jnp.where(hot, values[:, None], 0.0), axis=0)
    raw = butterfly_sum(per_vector, "vec")
    bias = jnp.clip(TIME_STEP_ROOT * raw, -1.0, 1.0)
    scales = TIME_STEP_ROOT * (aux_fields[0] - bias)
    ss = [pick(scales, source // KT) for source in sources]
    out = propagate(pad_rows(start), parts, rbs, cbs, ss)
    return out[:cols_local][None]


def solution(mesh):
    return jax.shard_map(
        shards,
        mesh=mesh,
        in_specs=(
            P("walker"),
            P("walker", "vec", None),
            P("walker", "vec", None),
            P(),
            P(("walker", "vec"), None, None),
            P(),
            P("walker", None),
        ),
        out_specs=P("walker", "vec", None),
        check_vma=False,
    )
```

```python
import functools

import jax
import jax.numpy as jnp
from jax import lax
from jax.experimental import pallas as pl
from jax.experimental.pallas import tpu as pltpu
from jax.sharding import PartitionSpec as P

KT = 4
TERMS = 3
TIME_STEP_ROOT = 0.1
ROWS = 32
INTERPRET = False


def shift_from(value, axis, steps):
    count = lax.axis_size(axis)
    return lax.ppermute(value, axis, [(i, i + steps) for i in range(count - steps)])


def butterfly_sum(value, axis):
    count = lax.axis_size(axis)
    step = 1
    while step < count:
        value = value + lax.ppermute(value, axis, [(i, i ^ step) for i in range(count)])
        step *= 2
    return value


def bias_kernel(*refs):
    count = len(STREAMS)
    rbs, cbs = refs[:count], refs[count:2 * count]
    pt_ref, g_ref = refs[2 * count], refs[2 * count + 1]
    parts = refs[2 * count + 2:3 * count + 2]
    outs = refs[3 * count + 2:4 * count + 2]
    m_ref = refs[-1]
    blocks, size, _ = m_ref.shape
    for a in range(blocks):
        m_ref[a] = jnp.dot(
            pt_ref[a * size:(a + 1) * size, :], g_ref[...], preferred_element_type=jnp.float32
        )

    def one(t, carry):
        for (_, low, high), rb_ref, cb_ref, part_ref, out_ref in zip(STREAMS, rbs, cbs, parts, outs):
            col = pl.multiple_of(cb_ref[t] * size, size)
            blk = m_ref[rb_ref[t], low:high, pl.ds(col, size)]
            prod = blk * part_ref[t, 0:high - low, :].astype(jnp.float32)
            out_ref[pl.ds(t, 1), :] = jnp.sum(prod, axis=0, keepdims=True)
        return carry

    lax.fori_loop(0, parts[0].shape[0], one, 0, unroll=2)


def tile_bias(panel_t, green, parts, rbs, cbs):
    tiles_total, _, size = parts[0].shape
    orbitals = green.shape[1]
    blocks = orbitals // size
    count = len(parts)
    smem = pl.BlockSpec(memory_space=pltpu.SMEM)
    vmem = pl.BlockSpec(memory_space=pltpu.VMEM)
    return pl.pallas_call(
        bias_kernel,
        out_shape=[jax.ShapeDtypeStruct((tiles_total, size), jnp.float32)] * count,
        in_specs=[smem] * (2 * count) + [vmem] * (2 + count),
        out_specs=[vmem] * count,
        scratch_shapes=[pltpu.VMEM((blocks, size, orbitals), jnp.float32)],
        compiler_params=pltpu.CompilerParams(vmem_limit_bytes=48 * 1024 * 1024),
        interpret=INTERPRET,
    )(*rbs, *cbs, panel_t, green, *parts)


def prop_kernel(*refs):
    count = len(STREAMS)
    rbs, cbs, ss = refs[:count], refs[count:2 * count], refs[2 * count:3 * count]
    x_ref = refs[3 * count]
    parts = refs[3 * count + 1:4 * count + 1]
    out_ref, hi_ref, lo_ref, y_ref = refs[4 * count + 1:]
    orbitals = hi_ref.shape[0]
    size = parts[0].shape[2]
    hi_ref[...] = jnp.zeros(hi_ref.shape, hi_ref.dtype)
    lo_ref[...] = jnp.zeros(lo_ref.shape, lo_ref.dtype)

    def build(t, carry):
        for (_, low, high), rb_ref, cb_ref, s_ref, part_ref in zip(STREAMS, rbs, cbs, ss, parts):
            rows = pl.ds(pl.multiple_of(rb_ref[t] * size + low, 16), high - low)
            cols = pl.ds(pl.multiple_of(cb_ref[t] * size, size), size)
            whole = (
                hi_ref[rows, cols].astype(jnp.float32)
                + lo_ref[rows, cols].astype(jnp.float32)
                + s_ref[t] * part_ref[t, 0:high - low, :].astype(jnp.float32)
            )
            upper = whole.astype(jnp.bfloat16)
            hi_ref[rows, cols] = upper
            lo_ref[rows, cols] = (whole - upper.astype(jnp.float32)).astype(jnp.bfloat16)
        return carry

    lax.fori_loop(0, parts[0].shape[0], build, 0)

    chunk = 512
    series = x_ref[...]
    running = series.astype(jnp.float32)
    for degree in range(1, TERMS + 1):
        for c in range(orbitals // chunk):
            span = slice(c * chunk, (c + 1) * chunk)
            y_ref[span, :] = jnp.dot(
                hi_ref[span, :], series, preferred_element_type=jnp.float32
            ) + jnp.dot(lo_ref[span, :], series, preferred_element_type=jnp.float32)
        series = (y_ref[...] / degree).astype(jnp.bfloat16)
        running = running + series.astype(jnp.float32)
    out_ref[...] = running.astype(out_ref.dtype)


def propagate(x0, parts, rbs, cbs, ss):
    size = parts[0].shape[2]
    orbitals, rows = x0.shape
    blocks = orbitals // size
    count = len(parts)
    smem = pl.BlockSpec(memory_space=pltpu.SMEM)
    vmem = pl.BlockSpec(memory_space=pltpu.VMEM)
    return pl.pallas_call(
        prop_kernel,
        out_shape=jax.ShapeDtypeStruct((orbitals, rows), jnp.bfloat16),
        in_specs=[smem] * (3 * count) + [vmem] * (1 + count),
        out_specs=vmem,
        scratch_shapes=[
            pltpu.VMEM((orbitals, orbitals), jnp.bfloat16),
            pltpu.VMEM((orbitals, orbitals), jnp.bfloat16),
            pltpu.VMEM((orbitals, rows), jnp.float32),
        ],
        compiler_params=pltpu.CompilerParams(vmem_limit_bytes=48 * 1024 * 1024),
        interpret=INTERPRET,
    )(*rbs, *cbs, *ss, x0, *parts)


STREAMS = (
    ((("walker", 16), ("walker", 8), ("walker", 4), ("vec", 4), ("walker", 2), ("vec", 2), ("vec", 1), ("walker", 1)), 0, 48),
    ((("vec", 2), ("vec", 1), ("walker", 16), ("walker", 8), ("walker", 4), ("vec", 4), ("walker", 2), ("walker", 1)), 48, 96),
    ((("vec", 4), ("walker", 2), ("vec", 2), ("vec", 1), ("walker", 16), ("walker", 8), ("walker", 4), ("walker", 1)), 96, 128),
)


def xor_gather(x, order):
    for axis, step in order:
        count = lax.axis_size(axis)
        other = lax.ppermute(x, axis, [(i, i ^ step) for i in range(count)])
        x = jnp.concatenate([x, other], axis=0)
    return x


def source_tiles(order):
    position = jnp.arange(2 ** len(order), dtype=jnp.int32)
    masks = {"walker": jnp.zeros_like(position), "vec": jnp.zeros_like(position)}
    for bit, (axis, step) in enumerate(order):
        masks[axis] = masks[axis] + ((position >> bit) & 1) * step
    walker = jnp.bitwise_xor(lax.axis_index("walker"), masks["walker"])
    vec = jnp.bitwise_xor(lax.axis_index("vec"), masks["vec"])
    return walker * lax.axis_size("vec") + vec


def pick(table, index):
    hot = index[:, None] == jnp.arange(table.shape[0], dtype=index.dtype)[None, :]
    return jnp.sum(jnp.where(hot, table[None, :], jnp.zeros((), table.dtype)), axis=1)


def pad_rows(x):
    return jnp.pad(x, ((0, ROWS - x.shape[0]), (0, 0)))


def shards(
    copy_counts, panels, inverse_intersection, trial_orbitals, chol_tiles, tile_blocks, aux_fields
):
    cols_local = panels.shape[1]
    walker_id = lax.axis_index("walker")
    vec_id = lax.axis_index("vec")
    vecs = lax.axis_size("vec")
    prev_panel = shift_from(panels, "walker", 1)
    prev_inverse = shift_from(inverse_intersection, "walker", 1)
    size = chol_tiles.shape[2]
    meta = jnp.zeros((1, 16, size), chol_tiles.dtype).at[0, 0, 0].set(copy_counts[0].astype(chol_tiles.dtype))
    parts, rbs, cbs, sources = [], [], [], []
    for index, (order, low, high) in enumerate(STREAMS):
        piece = chol_tiles[:, low:high]
        if index == len(STREAMS) - 1:
            piece = jnp.concatenate([piece, meta], axis=1)
        parts.append(xor_gather(piece, order))
        source = source_tiles(order)
        sources.append(source)
        rbs.append(pick(tile_blocks[:, 0], source))
        cbs.append(pick(tile_blocks[:, 1], source))
    last = STREAMS[-1]
    counts = parts[-1][:, last[2] - last[1], 0].astype(jnp.float32)
    source = sources[-1]
    before = (source % vecs == vec_id) & (source // vecs < walker_id)
    surplus = jnp.sum(jnp.where(before, counts, 0.0)) - walker_id.astype(jnp.float32)
    from_prev = surplus > 0.5

    green_own = jnp.dot(inverse_intersection[0], trial_orbitals, preferred_element_type=jnp.float32).astype(jnp.bfloat16)
    green_prev = jnp.dot(prev_inverse[0], trial_orbitals, preferred_element_type=jnp.float32).astype(jnp.bfloat16)
    start = jnp.where(from_prev, prev_panel[0], panels[0])
    green = jnp.where(from_prev, green_prev, green_own)
    partials = tile_bias(pad_rows(start).T, pad_rows(green), parts, rbs, cbs)
    vectors = tile_blocks.shape[0] // KT
    ids = jnp.concatenate([source // KT for source in sources])
    values = jnp.concatenate([partial.sum(axis=1) for partial in partials])
    hot = ids[:, None] == jnp.arange(vectors, dtype=ids.dtype)[None, :]
    per_vector = jnp.sum(jnp.where(hot, values[:, None], 0.0), axis=0)
    raw = butterfly_sum(per_vector, "vec")
    bias = jnp.clip(TIME_STEP_ROOT * raw, -1.0, 1.0)
    scales = TIME_STEP_ROOT * (aux_fields[0] - bias)
    ss = [pick(scales, source // KT) for source in sources]
    out = propagate(pad_rows(start).T, parts, rbs, cbs, ss)
    return out.T[:cols_local][None]


def solution(mesh):
    return jax.shard_map(
        shards,
        mesh=mesh,
        in_specs=(
            P("walker"),
            P("walker", "vec", None),
            P("walker", "vec", None),
            P(),
            P(("walker", "vec"), None, None),
            P(),
            P("walker", None),
        ),
        out_specs=P("walker", "vec", None),
        check_vma=False,
    )
```

```python
import functools

import jax
import jax.numpy as jnp
from jax import lax
from jax.experimental import pallas as pl
from jax.experimental.pallas import tpu as pltpu
from jax.sharding import PartitionSpec as P

KT = 4
TERMS = 3
TIME_STEP_ROOT = 0.1
ROWS = 32
INTERPRET = False


def shift_from(value, axis, steps):
    count = lax.axis_size(axis)
    return lax.ppermute(value, axis, [(i, i + steps) for i in range(count - steps)])


def butterfly_sum(value, axis):
    count = lax.axis_size(axis)
    step = 1
    while step < count:
        value = value + lax.ppermute(value, axis, [(i, i ^ step) for i in range(count)])
        step *= 2
    return value


def bias_kernel(*refs):
    count = len(STREAMS)
    rbs, cbs = refs[:count], refs[count:2 * count]
    pt_ref, g_ref = refs[2 * count], refs[2 * count + 1]
    parts = refs[2 * count + 2:3 * count + 2]
    outs = refs[3 * count + 2:4 * count + 2]
    m_ref = refs[-1]
    blocks, size, _ = m_ref.shape
    for a in range(blocks):
        m_ref[a] = jnp.dot(
            pt_ref[a * size:(a + 1) * size, :], g_ref[...], preferred_element_type=jnp.float32
        )

    def one(t, carry):
        for (_, low, high), rb_ref, cb_ref, part_ref, out_ref in zip(STREAMS, rbs, cbs, parts, outs):
            col = pl.multiple_of(cb_ref[t] * size, size)
            blk = m_ref[rb_ref[t], low:high, pl.ds(col, size)]
            prod = blk * part_ref[t, 0:high - low, :].astype(jnp.float32)
            out_ref[pl.ds(t, 1), :] = jnp.sum(prod, axis=0, keepdims=True)
        return carry

    lax.fori_loop(0, parts[0].shape[0], one, 0, unroll=2)


def tile_bias(panel_t, green, parts, rbs, cbs):
    tiles_total, _, size = parts[0].shape
    orbitals = green.shape[1]
    blocks = orbitals // size
    count = len(parts)
    smem = pl.BlockSpec(memory_space=pltpu.SMEM)
    vmem = pl.BlockSpec(memory_space=pltpu.VMEM)
    return pl.pallas_call(
        bias_kernel,
        out_shape=[jax.ShapeDtypeStruct((tiles_total, size), jnp.float32)] * count,
        in_specs=[smem] * (2 * count) + [vmem] * (2 + count),
        out_specs=[vmem] * count,
        scratch_shapes=[pltpu.VMEM((blocks, size, orbitals), jnp.float32)],
        compiler_params=pltpu.CompilerParams(vmem_limit_bytes=48 * 1024 * 1024),
        interpret=INTERPRET,
    )(*rbs, *cbs, panel_t, green, *parts)


def prop_kernel(*refs):
    count = len(STREAMS)
    rbs, cbs, ss = refs[:count], refs[count:2 * count], refs[2 * count:3 * count]
    x_ref = refs[3 * count]
    parts = refs[3 * count + 1:4 * count + 1]
    out_ref, hi_ref, lo_ref, y_ref = refs[4 * count + 1:]
    orbitals = hi_ref.shape[0]
    size = parts[0].shape[2]
    hi_ref[...] = jnp.zeros(hi_ref.shape, hi_ref.dtype)
    lo_ref[...] = jnp.zeros(lo_ref.shape, lo_ref.dtype)

    def build(t, carry):
        for (_, low, high), rb_ref, cb_ref, s_ref, part_ref in zip(STREAMS, rbs, cbs, ss, parts):
            rows = pl.ds(pl.multiple_of(rb_ref[t] * size + low, 16), high - low)
            cols = pl.ds(pl.multiple_of(cb_ref[t] * size, size), size)
            whole = (
                hi_ref[rows, cols].astype(jnp.float32)
                + lo_ref[rows, cols].astype(jnp.float32)
                + s_ref[t] * part_ref[t, 0:high - low, :].astype(jnp.float32)
            )
            upper = whole.astype(jnp.bfloat16)
            hi_ref[rows, cols] = upper
            lo_ref[rows, cols] = (whole - upper.astype(jnp.float32)).astype(jnp.bfloat16)
        return carry

    lax.fori_loop(0, parts[0].shape[0], build, 0)

    chunk = 512
    series = x_ref[...]
    running = series.astype(jnp.float32)
    for degree in range(1, TERMS + 1):
        for c in range(orbitals // chunk):
            span = slice(c * chunk, (c + 1) * chunk)
            y_ref[span, :] = jnp.dot(
                hi_ref[span, :], series, preferred_element_type=jnp.float32
            ) + jnp.dot(lo_ref[span, :], series, preferred_element_type=jnp.float32)
        series = (y_ref[...] / degree).astype(jnp.bfloat16)
        running = running + series.astype(jnp.float32)
    out_ref[...] = running.astype(out_ref.dtype)


def propagate(x0, parts, rbs, cbs, ss):
    size = parts[0].shape[2]
    orbitals, rows = x0.shape
    blocks = orbitals // size
    count = len(parts)
    smem = pl.BlockSpec(memory_space=pltpu.SMEM)
    vmem = pl.BlockSpec(memory_space=pltpu.VMEM)
    return pl.pallas_call(
        prop_kernel,
        out_shape=jax.ShapeDtypeStruct((orbitals, rows), jnp.bfloat16),
        in_specs=[smem] * (3 * count) + [vmem] * (1 + count),
        out_specs=vmem,
        scratch_shapes=[
            pltpu.VMEM((orbitals, orbitals), jnp.bfloat16),
            pltpu.VMEM((orbitals, orbitals), jnp.bfloat16),
            pltpu.VMEM((orbitals, rows), jnp.float32),
        ],
        compiler_params=pltpu.CompilerParams(vmem_limit_bytes=48 * 1024 * 1024),
        interpret=INTERPRET,
    )(*rbs, *cbs, *ss, x0, *parts)


STREAMS = ((None, 0, 128),)


def xor_gather(x, order):
    for axis, step in order:
        count = lax.axis_size(axis)
        other = lax.ppermute(x, axis, [(i, i ^ step) for i in range(count)])
        x = jnp.concatenate([x, other], axis=0)
    return x


def source_tiles(order):
    position = jnp.arange(2 ** len(order), dtype=jnp.int32)
    masks = {"walker": jnp.zeros_like(position), "vec": jnp.zeros_like(position)}
    for bit, (axis, step) in enumerate(order):
        masks[axis] = masks[axis] + ((position >> bit) & 1) * step
    walker = jnp.bitwise_xor(lax.axis_index("walker"), masks["walker"])
    vec = jnp.bitwise_xor(lax.axis_index("vec"), masks["vec"])
    return walker * lax.axis_size("vec") + vec


def pick(table, index):
    hot = index[:, None] == jnp.arange(table.shape[0], dtype=index.dtype)[None, :]
    return jnp.sum(jnp.where(hot, table[None, :], jnp.zeros((), table.dtype)), axis=1)


def pad_rows(x):
    return jnp.pad(x, ((0, ROWS - x.shape[0]), (0, 0)))


def shards(
    copy_counts, panels, inverse_intersection, trial_orbitals, chol_tiles, tile_blocks, aux_fields
):
    cols_local = panels.shape[1]
    walker_id = lax.axis_index("walker")
    vecs = lax.axis_size("vec")
    prev_panel = shift_from(panels, "walker", 1)
    prev_inverse = shift_from(inverse_intersection, "walker", 1)
    size = chol_tiles.shape[2]
    meta = jnp.zeros((1, 16, size), chol_tiles.dtype).at[0, 0, 0].set(copy_counts[0].astype(chol_tiles.dtype))
    payload = jnp.concatenate([chol_tiles, meta], axis=1)
    gathered = lax.all_gather(
        lax.all_gather(payload, "vec", axis=0, tiled=True), "walker", axis=0, tiled=True
    )
    tiles_rows = chol_tiles.shape[1]
    counts = gathered[::vecs, tiles_rows, 0].astype(jnp.float32)
    walkers = jnp.arange(counts.shape[0])
    surplus = jnp.sum(jnp.where(walkers < walker_id, counts, 0.0)) - walker_id.astype(jnp.float32)
    from_prev = surplus > 0.5
    rbs = [tile_blocks[:, 0]]
    cbs = [tile_blocks[:, 1]]
    parts = [gathered]

    green_own = jnp.dot(inverse_intersection[0], trial_orbitals, preferred_element_type=jnp.float32).astype(jnp.bfloat16)
    green_prev = jnp.dot(prev_inverse[0], trial_orbitals, preferred_element_type=jnp.float32).astype(jnp.bfloat16)
    start = jnp.where(from_prev, prev_panel[0], panels[0])
    green = jnp.where(from_prev, green_prev, green_own)
    partials = tile_bias(pad_rows(start).T, pad_rows(green), parts, rbs, cbs)
    vectors = tile_blocks.shape[0] // KT
    per_vector = partials[0].reshape(vectors, KT * size).sum(axis=1)
    raw = butterfly_sum(per_vector, "vec")
    bias = jnp.clip(TIME_STEP_ROOT * raw, -1.0, 1.0)
    scales = TIME_STEP_ROOT * (aux_fields[0] - bias)
    ss = [jnp.repeat(scales, KT)]
    out = propagate(pad_rows(start).T, parts, rbs, cbs, ss)
    return out.T[:cols_local][None]


def solution(mesh):
    return jax.shard_map(
        shards,
        mesh=mesh,
        in_specs=(
            P("walker"),
            P("walker", "vec", None),
            P("walker", "vec", None),
            P(),
            P(("walker", "vec"), None, None),
            P(),
            P("walker", None),
        ),
        out_specs=P("walker", "vec", None),
        check_vma=False,
    )
```

```python
import functools

import jax
import jax.numpy as jnp
from jax import lax
from jax.experimental import pallas as pl
from jax.experimental.pallas import tpu as pltpu
from jax.sharding import PartitionSpec as P

KT = 4
TERMS = 3
TIME_STEP_ROOT = 0.1
ROWS = 32
INTERPRET = False


def shift_from(value, axis, steps):
    count = lax.axis_size(axis)
    return lax.ppermute(value, axis, [(i, i + steps) for i in range(count - steps)])


def butterfly_sum(value, axis):
    count = lax.axis_size(axis)
    step = 1
    while step < count:
        value = value + lax.ppermute(value, axis, [(i, i ^ step) for i in range(count)])
        step *= 2
    return value


def bias_kernel(*refs):
    count = len(STREAMS)
    rbs, cbs = refs[:count], refs[count:2 * count]
    pt_ref, g_ref = refs[2 * count], refs[2 * count + 1]
    parts = refs[2 * count + 2:3 * count + 2]
    outs = refs[3 * count + 2:4 * count + 2]
    m_ref = refs[-1]
    blocks, size, _ = m_ref.shape
    for a in range(blocks):
        m_ref[a] = jnp.dot(
            pt_ref[a * size:(a + 1) * size, :], g_ref[...], preferred_element_type=jnp.float32
        )

    def one(t, carry):
        for (_, low, high), rb_ref, cb_ref, part_ref, out_ref in zip(STREAMS, rbs, cbs, parts, outs):
            col = pl.multiple_of(cb_ref[t] * size, size)
            blk = m_ref[rb_ref[t], low:high, pl.ds(col, size)]
            prod = blk * part_ref[t, 0:high - low, :].astype(jnp.float32)
            out_ref[pl.ds(t, 1), :] = jnp.sum(prod, axis=0, keepdims=True)
        return carry

    lax.fori_loop(0, parts[0].shape[0], one, 0, unroll=2)


def tile_bias(panel_t, green, parts, rbs, cbs):
    tiles_total, _, size = parts[0].shape
    orbitals = green.shape[1]
    blocks = orbitals // size
    count = len(parts)
    smem = pl.BlockSpec(memory_space=pltpu.SMEM)
    vmem = pl.BlockSpec(memory_space=pltpu.VMEM)
    return pl.pallas_call(
        bias_kernel,
        out_shape=[jax.ShapeDtypeStruct((tiles_total, size), jnp.float32)] * count,
        in_specs=[smem] * (2 * count) + [vmem] * (2 + count),
        out_specs=[vmem] * count,
        scratch_shapes=[pltpu.VMEM((blocks, size, orbitals), jnp.float32)],
        compiler_params=pltpu.CompilerParams(vmem_limit_bytes=48 * 1024 * 1024),
        interpret=INTERPRET,
    )(*rbs, *cbs, panel_t, green, *parts)


def prop_kernel(*refs):
    count = len(STREAMS)
    rbs, cbs, ss = refs[:count], refs[count:2 * count], refs[2 * count:3 * count]
    x_ref = refs[3 * count]
    parts = refs[3 * count + 1:4 * count + 1]
    out_ref, hi_ref, lo_ref, y_ref = refs[4 * count + 1:]
    orbitals = hi_ref.shape[0]
    size = parts[0].shape[2]
    hi_ref[...] = jnp.zeros(hi_ref.shape, hi_ref.dtype)
    lo_ref[...] = jnp.zeros(lo_ref.shape, lo_ref.dtype)

    def build(t, carry):
        for (_, low, high), rb_ref, cb_ref, s_ref, part_ref in zip(STREAMS, rbs, cbs, ss, parts):
            rows = pl.ds(pl.multiple_of(rb_ref[t] * size + low, 16), high - low)
            cols = pl.ds(pl.multiple_of(cb_ref[t] * size, size), size)
            whole = (
                hi_ref[rows, cols].astype(jnp.float32)
                + lo_ref[rows, cols].astype(jnp.float32)
                + s_ref[t] * part_ref[t, 0:high - low, :].astype(jnp.float32)
            )
            upper = whole.astype(jnp.bfloat16)
            hi_ref[rows, cols] = upper
            lo_ref[rows, cols] = (whole - upper.astype(jnp.float32)).astype(jnp.bfloat16)
        return carry

    lax.fori_loop(0, parts[0].shape[0], build, 0)

    chunk = 512
    series = x_ref[...]
    running = series.astype(jnp.float32)
    for degree in range(1, TERMS + 1):
        for c in range(orbitals // chunk):
            span = slice(c * chunk, (c + 1) * chunk)
            y_ref[span, :] = jnp.dot(
                hi_ref[span, :], series, preferred_element_type=jnp.float32
            ) + jnp.dot(lo_ref[span, :], series, preferred_element_type=jnp.float32)
        series = (y_ref[...] / degree).astype(jnp.bfloat16)
        running = running + series.astype(jnp.float32)
    out_ref[...] = running.astype(out_ref.dtype)


def propagate(x0, parts, rbs, cbs, ss):
    size = parts[0].shape[2]
    orbitals, rows = x0.shape
    blocks = orbitals // size
    count = len(parts)
    smem = pl.BlockSpec(memory_space=pltpu.SMEM)
    vmem = pl.BlockSpec(memory_space=pltpu.VMEM)
    return pl.pallas_call(
        prop_kernel,
        out_shape=jax.ShapeDtypeStruct((orbitals, rows), jnp.bfloat16),
        in_specs=[smem] * (3 * count) + [vmem] * (1 + count),
        out_specs=vmem,
        scratch_shapes=[
            pltpu.VMEM((orbitals, orbitals), jnp.bfloat16),
            pltpu.VMEM((orbitals, orbitals), jnp.bfloat16),
            pltpu.VMEM((orbitals, rows), jnp.float32),
        ],
        compiler_params=pltpu.CompilerParams(vmem_limit_bytes=48 * 1024 * 1024),
        interpret=INTERPRET,
    )(*rbs, *cbs, *ss, x0, *parts)


STREAMS = ((None, 0, 128),)


def xor_gather(x, order):
    for axis, step in order:
        count = lax.axis_size(axis)
        other = lax.ppermute(x, axis, [(i, i ^ step) for i in range(count)])
        x = jnp.concatenate([x, other], axis=0)
    return x


def source_tiles(order):
    position = jnp.arange(2 ** len(order), dtype=jnp.int32)
    masks = {"walker": jnp.zeros_like(position), "vec": jnp.zeros_like(position)}
    for bit, (axis, step) in enumerate(order):
        masks[axis] = masks[axis] + ((position >> bit) & 1) * step
    walker = jnp.bitwise_xor(lax.axis_index("walker"), masks["walker"])
    vec = jnp.bitwise_xor(lax.axis_index("vec"), masks["vec"])
    return walker * lax.axis_size("vec") + vec


def pick(table, index):
    hot = index[:, None] == jnp.arange(table.shape[0], dtype=index.dtype)[None, :]
    return jnp.sum(jnp.where(hot, table[None, :], jnp.zeros((), table.dtype)), axis=1)


def pad_rows(x):
    return jnp.pad(x, ((0, ROWS - x.shape[0]), (0, 0)))


def shards(
    copy_counts, panels, inverse_intersection, trial_orbitals, chol_tiles, tile_blocks, aux_fields
):
    cols_local = panels.shape[1]
    walker_id = lax.axis_index("walker")
    vecs = lax.axis_size("vec")
    prev_panel = shift_from(panels, "walker", 1)
    prev_inverse = shift_from(inverse_intersection, "walker", 1)
    size = chol_tiles.shape[2]
    meta = jnp.zeros((1, 16, size), chol_tiles.dtype).at[0, 0, 0].set(copy_counts[0].astype(chol_tiles.dtype))
    payload = jnp.concatenate([chol_tiles, meta], axis=1)
    order = (("vec", 4), ("vec", 2), ("vec", 1))
    gathered = lax.all_gather(xor_gather(payload, order), "walker", axis=0, tiled=True)
    tiles_rows = chol_tiles.shape[1]
    counts = gathered[::vecs, tiles_rows, 0].astype(jnp.float32)
    walkers = jnp.arange(counts.shape[0])
    surplus = jnp.sum(jnp.where(walkers < walker_id, counts, 0.0)) - walker_id.astype(jnp.float32)
    from_prev = surplus > 0.5
    local = source_tiles(order) % vecs
    source = (walkers[:, None] * vecs + local[None, :]).reshape(-1)
    rbs = [pick(tile_blocks[:, 0], source)]
    cbs = [pick(tile_blocks[:, 1], source)]
    parts = [gathered]

    green_own = jnp.dot(inverse_intersection[0], trial_orbitals, preferred_element_type=jnp.float32).astype(jnp.bfloat16)
    green_prev = jnp.dot(prev_inverse[0], trial_orbitals, preferred_element_type=jnp.float32).astype(jnp.bfloat16)
    start = jnp.where(from_prev, prev_panel[0], panels[0])
    green = jnp.where(from_prev, green_prev, green_own)
    partials = tile_bias(pad_rows(start).T, pad_rows(green), parts, rbs, cbs)
    vectors = tile_blocks.shape[0] // KT
    values = partials[0].sum(axis=1)
    hot = (source // KT)[:, None] == jnp.arange(vectors, dtype=source.dtype)[None, :]
    per_vector = jnp.sum(jnp.where(hot, values[:, None], 0.0), axis=0)
    raw = butterfly_sum(per_vector, "vec")
    bias = jnp.clip(TIME_STEP_ROOT * raw, -1.0, 1.0)
    scales = TIME_STEP_ROOT * (aux_fields[0] - bias)
    ss = [pick(scales, source // KT)]
    out = propagate(pad_rows(start).T, parts, rbs, cbs, ss)
    return out.T[:cols_local][None]


def solution(mesh):
    return jax.shard_map(
        shards,
        mesh=mesh,
        in_specs=(
            P("walker"),
            P("walker", "vec", None),
            P("walker", "vec", None),
            P(),
            P(("walker", "vec"), None, None),
            P(),
            P("walker", None),
        ),
        out_specs=P("walker", "vec", None),
        check_vma=False,
    )
```

```python
import functools

import jax
import jax.numpy as jnp
from jax import lax
from jax.experimental import pallas as pl
from jax.experimental.pallas import tpu as pltpu
from jax.sharding import PartitionSpec as P

KT = 4
TERMS = 3
TIME_STEP_ROOT = 0.1
ROWS = 32
INTERPRET = False


def shift_from(value, axis, steps):
    count = lax.axis_size(axis)
    return lax.ppermute(value, axis, [(i, i + steps) for i in range(count - steps)])


def butterfly_sum(value, axis):
    count = lax.axis_size(axis)
    step = 1
    while step < count:
        value = value + lax.ppermute(value, axis, [(i, i ^ step) for i in range(count)])
        step *= 2
    return value


def bias_kernel(*refs):
    count = len(STREAMS)
    rbs, cbs = refs[:count], refs[count:2 * count]
    pt_ref, g_ref = refs[2 * count], refs[2 * count + 1]
    parts = refs[2 * count + 2:3 * count + 2]
    outs = refs[3 * count + 2:4 * count + 2]
    m_ref = refs[-1]
    blocks, size, _ = m_ref.shape
    for a in range(blocks):
        m_ref[a] = jnp.dot(
            pt_ref[a * size:(a + 1) * size, :], g_ref[...], preferred_element_type=jnp.float32
        )

    def one(t, carry):
        for (_, low, high), rb_ref, cb_ref, part_ref, out_ref in zip(STREAMS, rbs, cbs, parts, outs):
            col = pl.multiple_of(cb_ref[t] * size, size)
            blk = m_ref[rb_ref[t], low:high, pl.ds(col, size)]
            prod = blk * part_ref[t, 0:high - low, :].astype(jnp.float32)
            out_ref[pl.ds(t, 1), :] = jnp.sum(prod, axis=0, keepdims=True)
        return carry

    lax.fori_loop(0, parts[0].shape[0], one, 0, unroll=2)


def tile_bias(panel_t, green, parts, rbs, cbs):
    tiles_total, _, size = parts[0].shape
    orbitals = green.shape[1]
    blocks = orbitals // size
    count = len(parts)
    smem = pl.BlockSpec(memory_space=pltpu.SMEM)
    vmem = pl.BlockSpec(memory_space=pltpu.VMEM)
    return pl.pallas_call(
        bias_kernel,
        out_shape=[jax.ShapeDtypeStruct((tiles_total, size), jnp.float32)] * count,
        in_specs=[smem] * (2 * count) + [vmem] * (2 + count),
        out_specs=[vmem] * count,
        scratch_shapes=[pltpu.VMEM((blocks, size, orbitals), jnp.float32)],
        compiler_params=pltpu.CompilerParams(vmem_limit_bytes=48 * 1024 * 1024),
        interpret=INTERPRET,
    )(*rbs, *cbs, panel_t, green, *parts)


def prop_kernel(*refs):
    count = len(STREAMS)
    rbs, cbs, ss = refs[:count], refs[count:2 * count], refs[2 * count:3 * count]
    x_ref = refs[3 * count]
    parts = refs[3 * count + 1:4 * count + 1]
    out_ref, hi_ref, lo_ref, y_ref = refs[4 * count + 1:]
    orbitals = hi_ref.shape[0]
    size = parts[0].shape[2]
    hi_ref[...] = jnp.zeros(hi_ref.shape, hi_ref.dtype)
    lo_ref[...] = jnp.zeros(lo_ref.shape, lo_ref.dtype)

    def build(t, carry):
        for (_, low, high), rb_ref, cb_ref, s_ref, part_ref in zip(STREAMS, rbs, cbs, ss, parts):
            rows = pl.ds(pl.multiple_of(rb_ref[t] * size + low, 16), high - low)
            cols = pl.ds(pl.multiple_of(cb_ref[t] * size, size), size)
            whole = (
                hi_ref[rows, cols].astype(jnp.float32)
                + lo_ref[rows, cols].astype(jnp.float32)
                + s_ref[t] * part_ref[t, 0:high - low, :].astype(jnp.float32)
            )
            upper = whole.astype(jnp.bfloat16)
            hi_ref[rows, cols] = upper
            lo_ref[rows, cols] = (whole - upper.astype(jnp.float32)).astype(jnp.bfloat16)
        return carry

    lax.fori_loop(0, parts[0].shape[0], build, 0)

    chunk = 512
    series = x_ref[...]
    running = series.astype(jnp.float32)
    for degree in range(1, TERMS + 1):
        for c in range(orbitals // chunk):
            span = slice(c * chunk, (c + 1) * chunk)
            y_ref[span, :] = jnp.dot(
                hi_ref[span, :], series, preferred_element_type=jnp.float32
            ) + jnp.dot(lo_ref[span, :], series, preferred_element_type=jnp.float32)
        series = (y_ref[...] / degree).astype(jnp.bfloat16)
        running = running + series.astype(jnp.float32)
    out_ref[...] = running.astype(out_ref.dtype)


def propagate(x0, parts, rbs, cbs, ss):
    size = parts[0].shape[2]
    orbitals, rows = x0.shape
    blocks = orbitals // size
    count = len(parts)
    smem = pl.BlockSpec(memory_space=pltpu.SMEM)
    vmem = pl.BlockSpec(memory_space=pltpu.VMEM)
    return pl.pallas_call(
        prop_kernel,
        out_shape=jax.ShapeDtypeStruct((orbitals, rows), jnp.bfloat16),
        in_specs=[smem] * (3 * count) + [vmem] * (1 + count),
        out_specs=vmem,
        scratch_shapes=[
            pltpu.VMEM((orbitals, orbitals), jnp.bfloat16),
            pltpu.VMEM((orbitals, orbitals), jnp.bfloat16),
            pltpu.VMEM((orbitals, rows), jnp.float32),
        ],
        compiler_params=pltpu.CompilerParams(vmem_limit_bytes=48 * 1024 * 1024),
        interpret=INTERPRET,
    )(*rbs, *cbs, *ss, x0, *parts)


STREAMS = ((None, 0, 128),)


def xor_gather(x, order):
    for axis, step in order:
        count = lax.axis_size(axis)
        other = lax.ppermute(x, axis, [(i, i ^ step) for i in range(count)])
        x = jnp.concatenate([x, other], axis=0)
    return x


def source_tiles(order):
    position = jnp.arange(2 ** len(order), dtype=jnp.int32)
    masks = {"walker": jnp.zeros_like(position), "vec": jnp.zeros_like(position)}
    for bit, (axis, step) in enumerate(order):
        masks[axis] = masks[axis] + ((position >> bit) & 1) * step
    walker = jnp.bitwise_xor(lax.axis_index("walker"), masks["walker"])
    vec = jnp.bitwise_xor(lax.axis_index("vec"), masks["vec"])
    return walker * lax.axis_size("vec") + vec


def pick(table, index):
    hot = index[:, None] == jnp.arange(table.shape[0], dtype=index.dtype)[None, :]
    return jnp.sum(jnp.where(hot, table[None, :], jnp.zeros((), table.dtype)), axis=1)


def pad_to(x, rows):
    return jnp.pad(x, ((0, rows - x.shape[0]), (0, 0)))


def pad_rows(x):
    return jnp.pad(x, ((0, ROWS - x.shape[0]), (0, 0)))


def shards(
    copy_counts, panels, inverse_intersection, trial_orbitals, chol_tiles, tile_blocks, aux_fields
):
    cols_local = panels.shape[1]
    walker_id = lax.axis_index("walker")
    vecs = lax.axis_size("vec")
    prev_panel = shift_from(panels, "walker", 1)
    prev_inverse = shift_from(inverse_intersection, "walker", 1)
    size = chol_tiles.shape[2]
    meta = jnp.zeros((1, 16, size), chol_tiles.dtype).at[0, 0, 0].set(copy_counts[0].astype(chol_tiles.dtype))
    payload = jnp.concatenate([chol_tiles, meta], axis=1)
    order = (("vec", 4), ("vec", 2), ("vec", 1))
    gathered = lax.all_gather(xor_gather(payload, order), "walker", axis=0, tiled=True)
    tiles_rows = chol_tiles.shape[1]
    counts = gathered[::vecs, tiles_rows, 0].astype(jnp.float32)
    walkers = jnp.arange(counts.shape[0])
    surplus = jnp.sum(jnp.where(walkers < walker_id, counts, 0.0)) - walker_id.astype(jnp.float32)
    from_prev = surplus > 0.5
    local = source_tiles(order) % vecs
    source = (walkers[:, None] * vecs + local[None, :]).reshape(-1)
    rbs = [pick(tile_blocks[:, 0], source)]
    cbs = [pick(tile_blocks[:, 1], source)]
    parts = [gathered]

    vec_order = (("vec", 1), ("vec", 2), ("vec", 4))
    both_panels = xor_gather(jnp.concatenate([panels, prev_panel], axis=0)[None], vec_order)
    both_inverse = xor_gather(jnp.concatenate([inverse_intersection, prev_inverse], axis=0)[None], vec_order)
    choice = jnp.where(from_prev, 1, 0)
    start_rows = lax.dynamic_index_in_dim(both_panels, choice, axis=1, keepdims=False)
    inverse_rows = lax.dynamic_index_in_dim(both_inverse, choice, axis=1, keepdims=False)
    full_rows = start_rows.shape[0] * start_rows.shape[1]
    start_all = start_rows.reshape(full_rows, -1)
    green_all = jnp.dot(
        inverse_rows.reshape(full_rows, -1), trial_orbitals, preferred_element_type=jnp.float32
    ).astype(jnp.bfloat16)
    start = jnp.where(from_prev, prev_panel[0], panels[0])
    partials = tile_bias(pad_to(start_all, 256).T, pad_to(green_all, 256), parts, rbs, cbs)
    vectors = tile_blocks.shape[0] // KT
    values = partials[0].sum(axis=1)
    hot = (source // KT)[:, None] == jnp.arange(vectors, dtype=source.dtype)[None, :]
    raw = jnp.sum(jnp.where(hot, values[:, None], 0.0), axis=0)
    bias = jnp.clip(TIME_STEP_ROOT * raw, -1.0, 1.0)
    scales = TIME_STEP_ROOT * (aux_fields[0] - bias)
    ss = [pick(scales, source // KT)]
    out = propagate(pad_rows(start).T, parts, rbs, cbs, ss)
    return out.T[:cols_local][None]


def solution(mesh):
    return jax.shard_map(
        shards,
        mesh=mesh,
        in_specs=(
            P("walker"),
            P("walker", "vec", None),
            P("walker", "vec", None),
            P(),
            P(("walker", "vec"), None, None),
            P(),
            P("walker", None),
        ),
        out_specs=P("walker", "vec", None),
        check_vma=False,
    )
```

```python
import functools

import jax
import jax.numpy as jnp
from jax import lax
from jax.experimental import pallas as pl
from jax.experimental.pallas import tpu as pltpu
from jax.sharding import PartitionSpec as P

KT = 4
TERMS = 3
TIME_STEP_ROOT = 0.1
ROWS = 32
INTERPRET = False


def shift_from(value, axis, steps):
    count = lax.axis_size(axis)
    return lax.ppermute(value, axis, [(i, i + steps) for i in range(count - steps)])


def butterfly_sum(value, axis):
    count = lax.axis_size(axis)
    step = 1
    while step < count:
        value = value + lax.ppermute(value, axis, [(i, i ^ step) for i in range(count)])
        step *= 2
    return value


def bias_kernel(*refs):
    count = len(STREAMS)
    rbs, cbs = refs[:count], refs[count:2 * count]
    pt_ref, g_ref = refs[2 * count], refs[2 * count + 1]
    parts = refs[2 * count + 2:3 * count + 2]
    outs = refs[3 * count + 2:4 * count + 2]
    m_ref = refs[-1]
    blocks, size, _ = m_ref.shape
    for a in range(blocks):
        m_ref[a] = jnp.dot(
            pt_ref[a * size:(a + 1) * size, :], g_ref[...], preferred_element_type=jnp.float32
        )

    def one(t, carry):
        for (_, low, high), rb_ref, cb_ref, part_ref, out_ref in zip(STREAMS, rbs, cbs, parts, outs):
            col = pl.multiple_of(cb_ref[t] * size, size)
            blk = m_ref[rb_ref[t], low:high, pl.ds(col, size)]
            prod = blk * part_ref[t, 0:high - low, :].astype(jnp.float32)
            out_ref[pl.ds(t, 1), :] = jnp.sum(prod, axis=0, keepdims=True)
        return carry

    lax.fori_loop(0, parts[0].shape[0], one, 0, unroll=2)


def tile_bias(panel_t, green, parts, rbs, cbs):
    tiles_total, _, size = parts[0].shape
    orbitals = green.shape[1]
    blocks = orbitals // size
    count = len(parts)
    smem = pl.BlockSpec(memory_space=pltpu.SMEM)
    vmem = pl.BlockSpec(memory_space=pltpu.VMEM)
    return pl.pallas_call(
        bias_kernel,
        out_shape=[jax.ShapeDtypeStruct((tiles_total, size), jnp.float32)] * count,
        in_specs=[smem] * (2 * count) + [vmem] * (2 + count),
        out_specs=[vmem] * count,
        scratch_shapes=[pltpu.VMEM((blocks, size, orbitals), jnp.float32)],
        compiler_params=pltpu.CompilerParams(vmem_limit_bytes=48 * 1024 * 1024),
        interpret=INTERPRET,
    )(*rbs, *cbs, panel_t, green, *parts)


def prop_kernel(*refs):
    count = len(STREAMS)
    rbs, cbs, ss = refs[:count], refs[count:2 * count], refs[2 * count:3 * count]
    x_ref = refs[3 * count]
    parts = refs[3 * count + 1:4 * count + 1]
    out_ref, hi_ref, lo_ref, y_ref = refs[4 * count + 1:]
    orbitals = hi_ref.shape[0]
    size = parts[0].shape[2]
    hi_ref[...] = jnp.zeros(hi_ref.shape, hi_ref.dtype)
    lo_ref[...] = jnp.zeros(lo_ref.shape, lo_ref.dtype)

    def build(t, carry):
        for (_, low, high), rb_ref, cb_ref, s_ref, part_ref in zip(STREAMS, rbs, cbs, ss, parts):
            rows = pl.ds(pl.multiple_of(rb_ref[t] * size + low, 16), high - low)
            cols = pl.ds(pl.multiple_of(cb_ref[t] * size, size), size)
            whole = (
                hi_ref[rows, cols].astype(jnp.float32)
                + lo_ref[rows, cols].astype(jnp.float32)
                + s_ref[t] * part_ref[t, 0:high - low, :].astype(jnp.float32)
            )
            upper = whole.astype(jnp.bfloat16)
            hi_ref[rows, cols] = upper
            lo_ref[rows, cols] = (whole - upper.astype(jnp.float32)).astype(jnp.bfloat16)
        return carry

    lax.fori_loop(0, parts[0].shape[0], build, 0)

    chunk = 512
    series = x_ref[...]
    running = series.astype(jnp.float32)
    for degree in range(1, TERMS + 1):
        for c in range(orbitals // chunk):
            span = slice(c * chunk, (c + 1) * chunk)
            y_ref[span, :] = jnp.dot(
                hi_ref[span, :], series, preferred_element_type=jnp.float32
            ) + jnp.dot(lo_ref[span, :], series, preferred_element_type=jnp.float32)
        series = (y_ref[...] / degree).astype(jnp.bfloat16)
        running = running + series.astype(jnp.float32)
    out_ref[...] = running.astype(out_ref.dtype)


def propagate(x0, parts, rbs, cbs, ss):
    size = parts[0].shape[2]
    orbitals, rows = x0.shape
    blocks = orbitals // size
    count = len(parts)
    smem = pl.BlockSpec(memory_space=pltpu.SMEM)
    vmem = pl.BlockSpec(memory_space=pltpu.VMEM)
    return pl.pallas_call(
        prop_kernel,
        out_shape=jax.ShapeDtypeStruct((orbitals, rows), jnp.bfloat16),
        in_specs=[smem] * (3 * count) + [vmem] * (1 + count),
        out_specs=vmem,
        scratch_shapes=[
            pltpu.VMEM((orbitals, orbitals), jnp.bfloat16),
            pltpu.VMEM((orbitals, orbitals), jnp.bfloat16),
            pltpu.VMEM((orbitals, rows), jnp.float32),
        ],
        compiler_params=pltpu.CompilerParams(vmem_limit_bytes=48 * 1024 * 1024),
        interpret=INTERPRET,
    )(*rbs, *cbs, *ss, x0, *parts)


STREAMS = ((None, 0, 128),)


def xor_gather(x, order):
    for axis, step in order:
        count = lax.axis_size(axis)
        other = lax.ppermute(x, axis, [(i, i ^ step) for i in range(count)])
        x = jnp.concatenate([x, other], axis=0)
    return x


def source_tiles(order):
    position = jnp.arange(2 ** len(order), dtype=jnp.int32)
    masks = {"walker": jnp.zeros_like(position), "vec": jnp.zeros_like(position)}
    for bit, (axis, step) in enumerate(order):
        masks[axis] = masks[axis] + ((position >> bit) & 1) * step
    walker = jnp.bitwise_xor(lax.axis_index("walker"), masks["walker"])
    vec = jnp.bitwise_xor(lax.axis_index("vec"), masks["vec"])
    return walker * lax.axis_size("vec") + vec


def pick(table, index):
    hot = index[:, None] == jnp.arange(table.shape[0], dtype=index.dtype)[None, :]
    return jnp.sum(jnp.where(hot, table[None, :], jnp.zeros((), table.dtype)), axis=1)


def pad_to(x, rows):
    return jnp.pad(x, ((0, rows - x.shape[0]), (0, 0)))


def pad_rows(x):
    return jnp.pad(x, ((0, ROWS - x.shape[0]), (0, 0)))


def shards(
    copy_counts, panels, inverse_intersection, trial_orbitals, chol_tiles, tile_blocks, aux_fields
):
    cols_local = panels.shape[1]
    walker_id = lax.axis_index("walker")
    vecs = lax.axis_size("vec")
    prev_panel = shift_from(panels, "walker", 1)
    prev_inverse = shift_from(inverse_intersection, "walker", 1)
    size = chol_tiles.shape[2]
    meta = jnp.zeros((1, 16, size), chol_tiles.dtype).at[0, 0, 0].set(copy_counts[0].astype(chol_tiles.dtype))
    payload = jnp.concatenate([chol_tiles, meta], axis=1)
    order = (("vec", 4), ("vec", 2), ("vec", 1))
    vec_tiles = xor_gather(payload, order)
    vec_tiles, panels_late, prev_late, inverse_late, prev_inverse_late = lax.optimization_barrier(
        (vec_tiles, panels, prev_panel, inverse_intersection, prev_inverse)
    )
    gathered = lax.all_gather(vec_tiles, "walker", axis=0, tiled=True)
    tiles_rows = chol_tiles.shape[1]
    counts = gathered[::vecs, tiles_rows, 0].astype(jnp.float32)
    walkers = jnp.arange(counts.shape[0])
    surplus = jnp.sum(jnp.where(walkers < walker_id, counts, 0.0)) - walker_id.astype(jnp.float32)
    from_prev = surplus > 0.5
    local = source_tiles(order) % vecs
    source = (walkers[:, None] * vecs + local[None, :]).reshape(-1)
    rbs = [pick(tile_blocks[:, 0], source)]
    cbs = [pick(tile_blocks[:, 1], source)]
    parts = [gathered]

    vec_order = (("vec", 1), ("vec", 2), ("vec", 4))
    both_panels = xor_gather(jnp.concatenate([panels_late, prev_late], axis=0)[None], vec_order)
    both_inverse = xor_gather(jnp.concatenate([inverse_late, prev_inverse_late], axis=0)[None], vec_order)
    choice = jnp.where(from_prev, 1, 0)
    start_rows = lax.dynamic_index_in_dim(both_panels, choice, axis=1, keepdims=False)
    inverse_rows = lax.dynamic_index_in_dim(both_inverse, choice, axis=1, keepdims=False)
    full_rows = start_rows.shape[0] * start_rows.shape[1]
    start_all = start_rows.reshape(full_rows, -1)
    green_all = jnp.dot(
        inverse_rows.reshape(full_rows, -1), trial_orbitals, preferred_element_type=jnp.float32
    ).astype(jnp.bfloat16)
    start = jnp.where(from_prev, prev_panel[0], panels[0])
    partials = tile_bias(pad_to(start_all, 256).T, pad_to(green_all, 256), parts, rbs, cbs)
    vectors = tile_blocks.shape[0] // KT
    values = partials[0].sum(axis=1)
    hot = (source // KT)[:, None] == jnp.arange(vectors, dtype=source.dtype)[None, :]
    raw = jnp.sum(jnp.where(hot, values[:, None], 0.0), axis=0)
    bias = jnp.clip(TIME_STEP_ROOT * raw, -1.0, 1.0)
    scales = TIME_STEP_ROOT * (aux_fields[0] - bias)
    ss = [pick(scales, source // KT)]
    out = propagate(pad_rows(start).T, parts, rbs, cbs, ss)
    return out.T[:cols_local][None]


def solution(mesh):
    return jax.shard_map(
        shards,
        mesh=mesh,
        in_specs=(
            P("walker"),
            P("walker", "vec", None),
            P("walker", "vec", None),
            P(),
            P(("walker", "vec"), None, None),
            P(),
            P("walker", None),
        ),
        out_specs=P("walker", "vec", None),
        check_vma=False,
    )
```

```python
import functools

import jax
import jax.numpy as jnp
from jax import lax
from jax.experimental import pallas as pl
from jax.experimental.pallas import tpu as pltpu
from jax.sharding import PartitionSpec as P

KT = 4
TERMS = 3
TIME_STEP_ROOT = 0.1
ROWS = 32
INTERPRET = False


def shift_from(value, axis, steps):
    count = lax.axis_size(axis)
    return lax.ppermute(value, axis, [(i, i + steps) for i in range(count - steps)])


def exchange_sum(value, axis):
    count = lax.axis_size(axis)
    me = lax.axis_index(axis)
    received = [value] + [
        lax.ppermute(value, axis, [(i, (i + step) % count) for i in range(count)])
        for step in range(1, count)
    ]
    stacked = jnp.stack(received)
    by_source = jnp.take(stacked, (me - jnp.arange(count)) % count, axis=0)
    total = by_source[0]
    for source in range(1, count):
        total = total + by_source[source]
    return total


def butterfly_sum(value, axis):
    count = lax.axis_size(axis)
    step = 1
    while step < count:
        value = value + lax.ppermute(value, axis, [(i, i ^ step) for i in range(count)])
        step *= 2
    return value


def bias_kernel(*refs):
    count = len(STREAMS)
    rbs, cbs = refs[:count], refs[count:2 * count]
    pt_ref, g_ref = refs[2 * count], refs[2 * count + 1]
    parts = refs[2 * count + 2:3 * count + 2]
    outs = refs[3 * count + 2:4 * count + 2]
    m_ref = refs[-1]
    blocks, size, _ = m_ref.shape
    for a in range(blocks):
        m_ref[a] = jnp.dot(
            pt_ref[a * size:(a + 1) * size, :], g_ref[...], preferred_element_type=jnp.float32
        )

    def one(t, carry):
        for (_, low, high), rb_ref, cb_ref, part_ref, out_ref in zip(STREAMS, rbs, cbs, parts, outs):
            col = pl.multiple_of(cb_ref[t] * size, size)
            blk = m_ref[rb_ref[t], low:high, pl.ds(col, size)]
            prod = blk * part_ref[t, 0:high - low, :].astype(jnp.float32)
            out_ref[pl.ds(t, 1), :] = jnp.sum(prod, axis=0, keepdims=True)
        return carry

    lax.fori_loop(0, parts[0].shape[0], one, 0, unroll=2)


def tile_bias(panel_t, green, parts, rbs, cbs):
    tiles_total, _, size = parts[0].shape
    orbitals = green.shape[1]
    blocks = orbitals // size
    count = len(parts)
    smem = pl.BlockSpec(memory_space=pltpu.SMEM)
    vmem = pl.BlockSpec(memory_space=pltpu.VMEM)
    return pl.pallas_call(
        bias_kernel,
        out_shape=[jax.ShapeDtypeStruct((tiles_total, size), jnp.float32)] * count,
        in_specs=[smem] * (2 * count) + [vmem] * (2 + count),
        out_specs=[vmem] * count,
        scratch_shapes=[pltpu.VMEM((blocks, size, orbitals), jnp.float32)],
        compiler_params=pltpu.CompilerParams(vmem_limit_bytes=48 * 1024 * 1024),
        interpret=INTERPRET,
    )(*rbs, *cbs, panel_t, green, *parts)


def prop_kernel(*refs):
    count = len(STREAMS)
    rbs, cbs, ss = refs[:count], refs[count:2 * count], refs[2 * count:3 * count]
    x_ref = refs[3 * count]
    parts = refs[3 * count + 1:4 * count + 1]
    out_ref, hi_ref, lo_ref, y_ref = refs[4 * count + 1:]
    orbitals = hi_ref.shape[0]
    size = parts[0].shape[2]
    hi_ref[...] = jnp.zeros(hi_ref.shape, hi_ref.dtype)
    lo_ref[...] = jnp.zeros(lo_ref.shape, lo_ref.dtype)

    def build(t, carry):
        for (_, low, high), rb_ref, cb_ref, s_ref, part_ref in zip(STREAMS, rbs, cbs, ss, parts):
            rows = pl.ds(pl.multiple_of(rb_ref[t] * size + low, 16), high - low)
            cols = pl.ds(pl.multiple_of(cb_ref[t] * size, size), size)
            whole = (
                hi_ref[rows, cols].astype(jnp.float32)
                + lo_ref[rows, cols].astype(jnp.float32)
                + s_ref[t] * part_ref[t, 0:high - low, :].astype(jnp.float32)
            )
            upper = whole.astype(jnp.bfloat16)
            hi_ref[rows, cols] = upper
            lo_ref[rows, cols] = (whole - upper.astype(jnp.float32)).astype(jnp.bfloat16)
        return carry

    lax.fori_loop(0, parts[0].shape[0], build, 0)

    chunk = 512
    series = x_ref[...]
    running = series.astype(jnp.float32)
    for degree in range(1, TERMS + 1):
        for c in range(orbitals // chunk):
            span = slice(c * chunk, (c + 1) * chunk)
            y_ref[span, :] = jnp.dot(
                hi_ref[span, :], series, preferred_element_type=jnp.float32
            ) + jnp.dot(lo_ref[span, :], series, preferred_element_type=jnp.float32)
        series = (y_ref[...] / degree).astype(jnp.bfloat16)
        running = running + series.astype(jnp.float32)
    out_ref[...] = running.astype(out_ref.dtype)


def propagate(x0, parts, rbs, cbs, ss):
    size = parts[0].shape[2]
    orbitals, rows = x0.shape
    blocks = orbitals // size
    count = len(parts)
    smem = pl.BlockSpec(memory_space=pltpu.SMEM)
    vmem = pl.BlockSpec(memory_space=pltpu.VMEM)
    return pl.pallas_call(
        prop_kernel,
        out_shape=jax.ShapeDtypeStruct((orbitals, rows), jnp.bfloat16),
        in_specs=[smem] * (3 * count) + [vmem] * (1 + count),
        out_specs=vmem,
        scratch_shapes=[
            pltpu.VMEM((orbitals, orbitals), jnp.bfloat16),
            pltpu.VMEM((orbitals, orbitals), jnp.bfloat16),
            pltpu.VMEM((orbitals, rows), jnp.float32),
        ],
        compiler_params=pltpu.CompilerParams(vmem_limit_bytes=48 * 1024 * 1024),
        interpret=INTERPRET,
    )(*rbs, *cbs, *ss, x0, *parts)


STREAMS = ((None, 0, 128),)


def xor_gather(x, order):
    for axis, step in order:
        count = lax.axis_size(axis)
        other = lax.ppermute(x, axis, [(i, i ^ step) for i in range(count)])
        x = jnp.concatenate([x, other], axis=0)
    return x


def source_tiles(order):
    position = jnp.arange(2 ** len(order), dtype=jnp.int32)
    masks = {"walker": jnp.zeros_like(position), "vec": jnp.zeros_like(position)}
    for bit, (axis, step) in enumerate(order):
        masks[axis] = masks[axis] + ((position >> bit) & 1) * step
    walker = jnp.bitwise_xor(lax.axis_index("walker"), masks["walker"])
    vec = jnp.bitwise_xor(lax.axis_index("vec"), masks["vec"])
    return walker * lax.axis_size("vec") + vec


def pick(table, index):
    hot = index[:, None] == jnp.arange(table.shape[0], dtype=index.dtype)[None, :]
    return jnp.sum(jnp.where(hot, table[None, :], jnp.zeros((), table.dtype)), axis=1)


def pad_rows(x):
    return jnp.pad(x, ((0, ROWS - x.shape[0]), (0, 0)))


def shards(
    copy_counts, panels, inverse_intersection, trial_orbitals, chol_tiles, tile_blocks, aux_fields
):
    cols_local = panels.shape[1]
    walker_id = lax.axis_index("walker")
    vecs = lax.axis_size("vec")
    prev_panel = shift_from(panels, "walker", 1)
    prev_inverse = shift_from(inverse_intersection, "walker", 1)
    size = chol_tiles.shape[2]
    meta = jnp.zeros((1, 16, size), chol_tiles.dtype).at[0, 0, 0].set(copy_counts[0].astype(chol_tiles.dtype))
    payload = jnp.concatenate([chol_tiles, meta], axis=1)
    order = (("vec", 4), ("vec", 2), ("vec", 1))
    gathered = lax.all_gather(xor_gather(payload, order), "walker", axis=0, tiled=True)
    tiles_rows = chol_tiles.shape[1]
    counts = gathered[::vecs, tiles_rows, 0].astype(jnp.float32)
    walkers = jnp.arange(counts.shape[0])
    surplus = jnp.sum(jnp.where(walkers < walker_id, counts, 0.0)) - walker_id.astype(jnp.float32)
    from_prev = surplus > 0.5
    local = source_tiles(order) % vecs
    source = (walkers[:, None] * vecs + local[None, :]).reshape(-1)
    rbs = [pick(tile_blocks[:, 0], source)]
    cbs = [pick(tile_blocks[:, 1], source)]
    parts = [gathered]

    green_own = jnp.dot(inverse_intersection[0], trial_orbitals, preferred_element_type=jnp.float32).astype(jnp.bfloat16)
    green_prev = jnp.dot(prev_inverse[0], trial_orbitals, preferred_element_type=jnp.float32).astype(jnp.bfloat16)
    start = jnp.where(from_prev, prev_panel[0], panels[0])
    green = jnp.where(from_prev, green_prev, green_own)
    partials = tile_bias(pad_rows(start).T, pad_rows(green), parts, rbs, cbs)
    vectors = tile_blocks.shape[0] // KT
    values = partials[0].sum(axis=1)
    hot = (source // KT)[:, None] == jnp.arange(vectors, dtype=source.dtype)[None, :]
    per_vector = jnp.sum(jnp.where(hot, values[:, None], 0.0), axis=0)
    raw = exchange_sum(per_vector, "vec")
    bias = jnp.clip(TIME_STEP_ROOT * raw, -1.0, 1.0)
    scales = TIME_STEP_ROOT * (aux_fields[0] - bias)
    ss = [pick(scales, source // KT)]
    out = propagate(pad_rows(start).T, parts, rbs, cbs, ss)
    return out.T[:cols_local][None]


def solution(mesh):
    return jax.shard_map(
        shards,
        mesh=mesh,
        in_specs=(
            P("walker"),
            P("walker", "vec", None),
            P("walker", "vec", None),
            P(),
            P(("walker", "vec"), None, None),
            P(),
            P("walker", None),
        ),
        out_specs=P("walker", "vec", None),
        check_vma=False,
    )
```

```python
import functools

import jax
import jax.numpy as jnp
from jax import lax
from jax.experimental import pallas as pl
from jax.experimental.pallas import tpu as pltpu
from jax.sharding import PartitionSpec as P

KT = 4
TERMS = 3
TIME_STEP_ROOT = 0.1
ROWS = 32
INTERPRET = False


def shift_from(value, axis, steps):
    count = lax.axis_size(axis)
    return lax.ppermute(value, axis, [(i, i + steps) for i in range(count - steps)])


def butterfly_sum(value, axis):
    count = lax.axis_size(axis)
    step = 1
    while step < count:
        value = value + lax.ppermute(value, axis, [(i, i ^ step) for i in range(count)])
        step *= 2
    return value


CHUNK = 32


def bias_kernel(rb_ref, cb_ref, pt_ref, g_ref, part_ref, out_ref, m_ref):
    step = pl.program_id(0)
    blocks, size, _ = m_ref.shape
    chunk = part_ref.shape[0]

    @pl.when(step == 0)
    def _():
        for a in range(blocks):
            m_ref[a] = jnp.dot(
                pt_ref[a * size:(a + 1) * size, :], g_ref[...], preferred_element_type=jnp.float32
            )

    def one(j, carry):
        t = step * chunk + j
        col = pl.multiple_of(cb_ref[t] * size, size)
        blk = m_ref[rb_ref[t], :, pl.ds(col, size)]
        prod = blk * part_ref[j, 0:size, :].astype(jnp.float32)
        out_ref[pl.ds(j, 1), :] = jnp.sum(prod, axis=0, keepdims=True)
        return carry

    lax.fori_loop(0, chunk, one, 0, unroll=2)


def tile_bias(panel_t, green, parts, rbs, cbs):
    part = parts[0]
    tiles_total, rows, size = part.shape
    orbitals = green.shape[1]
    blocks = orbitals // size
    smem = pl.BlockSpec(memory_space=pltpu.SMEM)
    return [pl.pallas_call(
        bias_kernel,
        out_shape=jax.ShapeDtypeStruct((tiles_total, size), jnp.float32),
        grid=(tiles_total // CHUNK,),
        in_specs=[
            smem,
            smem,
            pl.BlockSpec(panel_t.shape, lambda i: (0, 0)),
            pl.BlockSpec(green.shape, lambda i: (0, 0)),
            pl.BlockSpec((CHUNK, rows, size), lambda i: (i, 0, 0)),
        ],
        out_specs=pl.BlockSpec((CHUNK, size), lambda i: (i, 0)),
        scratch_shapes=[pltpu.VMEM((blocks, size, orbitals), jnp.float32)],
        compiler_params=pltpu.CompilerParams(
            dimension_semantics=("arbitrary",), vmem_limit_bytes=48 * 1024 * 1024
        ),
        interpret=INTERPRET,
    )(rbs[0], cbs[0], panel_t, green, part)]


def prop_kernel(rb_ref, cb_ref, s_ref, x_ref, part_ref, out_ref, hi_ref, lo_ref, y_ref):
    step = pl.program_id(0)
    orbitals = hi_ref.shape[0]
    size = part_ref.shape[2]
    chunk = part_ref.shape[0]

    @pl.when(step == 0)
    def _():
        hi_ref[...] = jnp.zeros(hi_ref.shape, hi_ref.dtype)
        lo_ref[...] = jnp.zeros(lo_ref.shape, lo_ref.dtype)

    def build(j, carry):
        t = step * chunk + j
        rows = pl.ds(pl.multiple_of(rb_ref[t] * size, size), size)
        cols = pl.ds(pl.multiple_of(cb_ref[t] * size, size), size)
        whole = (
            hi_ref[rows, cols].astype(jnp.float32)
            + lo_ref[rows, cols].astype(jnp.float32)
            + s_ref[t] * part_ref[j, 0:size, :].astype(jnp.float32)
        )
        upper = whole.astype(jnp.bfloat16)
        hi_ref[rows, cols] = upper
        lo_ref[rows, cols] = (whole - upper.astype(jnp.float32)).astype(jnp.bfloat16)
        return carry

    lax.fori_loop(0, chunk, build, 0)

    @pl.when(step == pl.num_programs(0) - 1)
    def _():
        span_rows = 512
        series = x_ref[...]
        running = series.astype(jnp.float32)
        for degree in range(1, TERMS + 1):
            for c in range(orbitals // span_rows):
                span = slice(c * span_rows, (c + 1) * span_rows)
                y_ref[span, :] = jnp.dot(
                    hi_ref[span, :], series, preferred_element_type=jnp.float32
                ) + jnp.dot(lo_ref[span, :], series, preferred_element_type=jnp.float32)
            series = (y_ref[...] / degree).astype(jnp.bfloat16)
            running = running + series.astype(jnp.float32)
        out_ref[...] = running.astype(out_ref.dtype)


def propagate(x0, parts, rbs, cbs, ss):
    part = parts[0]
    tiles_total, rows, size = part.shape
    orbitals, width = x0.shape
    smem = pl.BlockSpec(memory_space=pltpu.SMEM)
    return pl.pallas_call(
        prop_kernel,
        out_shape=jax.ShapeDtypeStruct((orbitals, width), jnp.bfloat16),
        grid=(tiles_total // CHUNK,),
        in_specs=[
            smem,
            smem,
            smem,
            pl.BlockSpec(x0.shape, lambda i: (0, 0)),
            pl.BlockSpec((CHUNK, rows, size), lambda i: (i, 0, 0)),
        ],
        out_specs=pl.BlockSpec((orbitals, width), lambda i: (0, 0)),
        scratch_shapes=[
            pltpu.VMEM((orbitals, orbitals), jnp.bfloat16),
            pltpu.VMEM((orbitals, orbitals), jnp.bfloat16),
            pltpu.VMEM((orbitals, width), jnp.float32),
        ],
        compiler_params=pltpu.CompilerParams(
            dimension_semantics=("arbitrary",), vmem_limit_bytes=48 * 1024 * 1024
        ),
        interpret=INTERPRET,
    )(rbs[0], cbs[0], ss[0], x0, part)


STREAMS = ((None, 0, 128),)


def xor_gather(x, order):
    for axis, step in order:
        count = lax.axis_size(axis)
        other = lax.ppermute(x, axis, [(i, i ^ step) for i in range(count)])
        x = jnp.concatenate([x, other], axis=0)
    return x


def source_tiles(order):
    position = jnp.arange(2 ** len(order), dtype=jnp.int32)
    masks = {"walker": jnp.zeros_like(position), "vec": jnp.zeros_like(position)}
    for bit, (axis, step) in enumerate(order):
        masks[axis] = masks[axis] + ((position >> bit) & 1) * step
    walker = jnp.bitwise_xor(lax.axis_index("walker"), masks["walker"])
    vec = jnp.bitwise_xor(lax.axis_index("vec"), masks["vec"])
    return walker * lax.axis_size("vec") + vec


def pick(table, index):
    hot = index[:, None] == jnp.arange(table.shape[0], dtype=index.dtype)[None, :]
    return jnp.sum(jnp.where(hot, table[None, :], jnp.zeros((), table.dtype)), axis=1)


def pad_rows(x):
    return jnp.pad(x, ((0, ROWS - x.shape[0]), (0, 0)))


def shards(
    copy_counts, panels, inverse_intersection, trial_orbitals, chol_tiles, tile_blocks, aux_fields
):
    cols_local = panels.shape[1]
    walker_id = lax.axis_index("walker")
    vecs = lax.axis_size("vec")
    prev_panel = shift_from(panels, "walker", 1)
    prev_inverse = shift_from(inverse_intersection, "walker", 1)
    size = chol_tiles.shape[2]
    meta = jnp.zeros((1, 16, size), chol_tiles.dtype).at[0, 0, 0].set(copy_counts[0].astype(chol_tiles.dtype))
    payload = jnp.concatenate([chol_tiles, meta], axis=1)
    order = (("vec", 4), ("vec", 2), ("vec", 1))
    gathered = lax.all_gather(xor_gather(payload, order), "walker", axis=0, tiled=True)
    tiles_rows = chol_tiles.shape[1]
    counts = gathered[::vecs, tiles_rows, 0].astype(jnp.float32)
    walkers = jnp.arange(counts.shape[0])
    surplus = jnp.sum(jnp.where(walkers < walker_id, counts, 0.0)) - walker_id.astype(jnp.float32)
    from_prev = surplus > 0.5
    local = source_tiles(order) % vecs
    source = (walkers[:, None] * vecs + local[None, :]).reshape(-1)
    rbs = [pick(tile_blocks[:, 0], source)]
    cbs = [pick(tile_blocks[:, 1], source)]
    parts = [gathered]

    green_own = jnp.dot(inverse_intersection[0], trial_orbitals, preferred_element_type=jnp.float32).astype(jnp.bfloat16)
    green_prev = jnp.dot(prev_inverse[0], trial_orbitals, preferred_element_type=jnp.float32).astype(jnp.bfloat16)
    start = jnp.where(from_prev, prev_panel[0], panels[0])
    green = jnp.where(from_prev, green_prev, green_own)
    partials = tile_bias(pad_rows(start).T, pad_rows(green), parts, rbs, cbs)
    vectors = tile_blocks.shape[0] // KT
    values = partials[0].sum(axis=1)
    hot = (source // KT)[:, None] == jnp.arange(vectors, dtype=source.dtype)[None, :]
    per_vector = jnp.sum(jnp.where(hot, values[:, None], 0.0), axis=0)
    raw = butterfly_sum(per_vector, "vec")
    bias = jnp.clip(TIME_STEP_ROOT * raw, -1.0, 1.0)
    scales = TIME_STEP_ROOT * (aux_fields[0] - bias)
    ss = [pick(scales, source // KT)]
    out = propagate(pad_rows(start).T, parts, rbs, cbs, ss)
    return out.T[:cols_local][None]


def solution(mesh):
    return jax.shard_map(
        shards,
        mesh=mesh,
        in_specs=(
            P("walker"),
            P("walker", "vec", None),
            P("walker", "vec", None),
            P(),
            P(("walker", "vec"), None, None),
            P(),
            P("walker", None),
        ),
        out_specs=P("walker", "vec", None),
        check_vma=False,
    )
```

```python
import functools

import jax
import jax.numpy as jnp
from jax import lax
from jax.experimental import pallas as pl
from jax.experimental.pallas import tpu as pltpu
from jax.sharding import PartitionSpec as P

KT = 4
TERMS = 3
TIME_STEP_ROOT = 0.1
ROWS = 32
INTERPRET = False


def shift_from(value, axis, steps):
    count = lax.axis_size(axis)
    return lax.ppermute(value, axis, [(i, i + steps) for i in range(count - steps)])


def butterfly_sum(value, axis):
    count = lax.axis_size(axis)
    step = 1
    while step < count:
        value = value + lax.ppermute(value, axis, [(i, i ^ step) for i in range(count)])
        step *= 2
    return value


CHUNK = 32


def bias_kernel(rb_ref, cb_ref, pt_ref, g_ref, part_ref, out_ref, m_ref):
    step = pl.program_id(0)
    blocks, size, _ = m_ref.shape
    chunk = part_ref.shape[0]

    @pl.when(step == 0)
    def _():
        for a in range(blocks):
            m_ref[a] = jnp.dot(
                pt_ref[a * size:(a + 1) * size, :], g_ref[...], preferred_element_type=jnp.float32
            )

    def one(j, carry):
        t = step * chunk + j
        col = pl.multiple_of(cb_ref[t] * size, size)
        blk = m_ref[rb_ref[t], :, pl.ds(col, size)]
        prod = blk * part_ref[j, 0:size, :].astype(jnp.float32)
        out_ref[pl.ds(j, 1), :] = jnp.sum(prod, axis=0, keepdims=True)
        return carry

    lax.fori_loop(0, chunk, one, 0, unroll=2)


def tile_bias(panel_t, green, parts, rbs, cbs):
    part = parts[0]
    tiles_total, rows, size = part.shape
    orbitals = green.shape[1]
    blocks = orbitals // size
    smem = pl.BlockSpec(memory_space=pltpu.SMEM)
    return [pl.pallas_call(
        bias_kernel,
        out_shape=jax.ShapeDtypeStruct((tiles_total, size), jnp.float32),
        grid=(tiles_total // CHUNK,),
        in_specs=[
            smem,
            smem,
            pl.BlockSpec(panel_t.shape, lambda i: (0, 0)),
            pl.BlockSpec(green.shape, lambda i: (0, 0)),
            pl.BlockSpec((CHUNK, rows, size), lambda i: (i, 0, 0)),
        ],
        out_specs=pl.BlockSpec((CHUNK, size), lambda i: (i, 0)),
        scratch_shapes=[pltpu.VMEM((blocks, size, orbitals), jnp.float32)],
        compiler_params=pltpu.CompilerParams(
            dimension_semantics=("arbitrary",), vmem_limit_bytes=48 * 1024 * 1024
        ),
        interpret=INTERPRET,
    )(rbs[0], cbs[0], panel_t, green, part)]


def prop_kernel(rb_ref, cb_ref, s_ref, x_ref, part_ref, out_ref, hi_ref, lo_ref, y_ref):
    step = pl.program_id(0)
    orbitals = hi_ref.shape[0]
    size = part_ref.shape[2]
    chunk = part_ref.shape[0]

    @pl.when(step == 0)
    def _():
        hi_ref[...] = jnp.zeros(hi_ref.shape, hi_ref.dtype)
        lo_ref[...] = jnp.zeros(lo_ref.shape, lo_ref.dtype)

    def build(j, carry):
        t = step * chunk + j
        rows = pl.ds(pl.multiple_of(rb_ref[t] * size, size), size)
        cols = pl.ds(pl.multiple_of(cb_ref[t] * size, size), size)
        whole = (
            hi_ref[rows, cols].astype(jnp.float32)
            + lo_ref[rows, cols].astype(jnp.float32)
            + s_ref[t] * part_ref[j, 0:size, :].astype(jnp.float32)
        )
        upper = whole.astype(jnp.bfloat16)
        hi_ref[rows, cols] = upper
        lo_ref[rows, cols] = (whole - upper.astype(jnp.float32)).astype(jnp.bfloat16)
        return carry

    lax.fori_loop(0, chunk, build, 0)

    @pl.when(step == pl.num_programs(0) - 1)
    def _():
        span_rows = 512
        series = x_ref[...]
        running = series.astype(jnp.float32)
        for degree in range(1, TERMS + 1):
            for c in range(orbitals // span_rows):
                span = slice(c * span_rows, (c + 1) * span_rows)
                y_ref[span, :] = jnp.dot(
                    hi_ref[span, :], series, preferred_element_type=jnp.float32
                ) + jnp.dot(lo_ref[span, :], series, preferred_element_type=jnp.float32)
            series = (y_ref[...] / degree).astype(jnp.bfloat16)
            running = running + series.astype(jnp.float32)
        out_ref[...] = running.astype(out_ref.dtype)


def propagate(x0, parts, rbs, cbs, ss):
    part = parts[0]
    tiles_total, rows, size = part.shape
    orbitals, width = x0.shape
    smem = pl.BlockSpec(memory_space=pltpu.SMEM)
    return pl.pallas_call(
        prop_kernel,
        out_shape=jax.ShapeDtypeStruct((orbitals, width), jnp.bfloat16),
        grid=(tiles_total // CHUNK,),
        in_specs=[
            smem,
            smem,
            smem,
            pl.BlockSpec(x0.shape, lambda i: (0, 0)),
            pl.BlockSpec((CHUNK, rows, size), lambda i: (i, 0, 0)),
        ],
        out_specs=pl.BlockSpec((orbitals, width), lambda i: (0, 0)),
        scratch_shapes=[
            pltpu.VMEM((orbitals, orbitals), jnp.bfloat16),
            pltpu.VMEM((orbitals, orbitals), jnp.bfloat16),
            pltpu.VMEM((orbitals, width), jnp.float32),
        ],
        compiler_params=pltpu.CompilerParams(
            dimension_semantics=("arbitrary",), vmem_limit_bytes=48 * 1024 * 1024
        ),
        interpret=INTERPRET,
    )(rbs[0], cbs[0], ss[0], x0, part)


STREAMS = ((None, 0, 128),)


def xor_gather(x, order):
    for axis, step in order:
        count = lax.axis_size(axis)
        other = lax.ppermute(x, axis, [(i, i ^ step) for i in range(count)])
        x = jnp.concatenate([x, other], axis=0)
    return x


def source_tiles(order):
    position = jnp.arange(2 ** len(order), dtype=jnp.int32)
    masks = {"walker": jnp.zeros_like(position), "vec": jnp.zeros_like(position)}
    for bit, (axis, step) in enumerate(order):
        masks[axis] = masks[axis] + ((position >> bit) & 1) * step
    walker = jnp.bitwise_xor(lax.axis_index("walker"), masks["walker"])
    vec = jnp.bitwise_xor(lax.axis_index("vec"), masks["vec"])
    return walker * lax.axis_size("vec") + vec


def pick(table, index):
    hot = index[:, None] == jnp.arange(table.shape[0], dtype=index.dtype)[None, :]
    return jnp.sum(jnp.where(hot, table[None, :], jnp.zeros((), table.dtype)), axis=1)


def pad_rows(x):
    return jnp.pad(x, ((0, ROWS - x.shape[0]), (0, 0)))


def shards(
    copy_counts, panels, inverse_intersection, trial_orbitals, chol_tiles, tile_blocks, aux_fields
):
    cols_local = panels.shape[1]
    walker_id = lax.axis_index("walker")
    vecs = lax.axis_size("vec")
    prev_panel = shift_from(panels, "walker", 1)
    prev_inverse = shift_from(inverse_intersection, "walker", 1)
    size = chol_tiles.shape[2]
    meta = jnp.zeros((1, 16, size), chol_tiles.dtype).at[0, 0, 0].set(copy_counts[0].astype(chol_tiles.dtype))
    payload = jnp.concatenate([chol_tiles, meta], axis=1)
    vec_id = lax.axis_index("vec")
    pieces = [payload] + [
        lax.ppermute(payload, "vec", [(i, (i + step) % vecs) for i in range(vecs)])
        for step in range(1, vecs)
    ]
    gathered = lax.all_gather(jnp.concatenate(pieces, axis=0), "walker", axis=0, tiled=True)
    tiles_rows = chol_tiles.shape[1]
    counts = gathered[::vecs, tiles_rows, 0].astype(jnp.float32)
    walkers = jnp.arange(counts.shape[0])
    surplus = jnp.sum(jnp.where(walkers < walker_id, counts, 0.0)) - walker_id.astype(jnp.float32)
    from_prev = surplus > 0.5
    local = (vec_id - jnp.arange(vecs, dtype=jnp.int32)) % vecs
    source = (walkers[:, None] * vecs + local[None, :]).reshape(-1)
    rbs = [pick(tile_blocks[:, 0], source)]
    cbs = [pick(tile_blocks[:, 1], source)]
    parts = [gathered]

    green_own = jnp.dot(inverse_intersection[0], trial_orbitals, preferred_element_type=jnp.float32).astype(jnp.bfloat16)
    green_prev = jnp.dot(prev_inverse[0], trial_orbitals, preferred_element_type=jnp.float32).astype(jnp.bfloat16)
    start = jnp.where(from_prev, prev_panel[0], panels[0])
    green = jnp.where(from_prev, green_prev, green_own)
    partials = tile_bias(pad_rows(start).T, pad_rows(green), parts, rbs, cbs)
    vectors = tile_blocks.shape[0] // KT
    values = partials[0].sum(axis=1)
    hot = (source // KT)[:, None] == jnp.arange(vectors, dtype=source.dtype)[None, :]
    per_vector = jnp.sum(jnp.where(hot, values[:, None], 0.0), axis=0)
    raw = butterfly_sum(per_vector, "vec")
    bias = jnp.clip(TIME_STEP_ROOT * raw, -1.0, 1.0)
    scales = TIME_STEP_ROOT * (aux_fields[0] - bias)
    ss = [pick(scales, source // KT)]
    out = propagate(pad_rows(start).T, parts, rbs, cbs, ss)
    return out.T[:cols_local][None]


def solution(mesh):
    return jax.shard_map(
        shards,
        mesh=mesh,
        in_specs=(
            P("walker"),
            P("walker", "vec", None),
            P("walker", "vec", None),
            P(),
            P(("walker", "vec"), None, None),
            P(),
            P("walker", None),
        ),
        out_specs=P("walker", "vec", None),
        check_vma=False,
    )
```

```python
import functools

import jax
import jax.numpy as jnp
from jax import lax
from jax.experimental import pallas as pl
from jax.experimental.pallas import tpu as pltpu
from jax.sharding import PartitionSpec as P

KT = 4
TERMS = 3
TIME_STEP_ROOT = 0.1
ROWS = 32
INTERPRET = False


def shift_from(value, axis, steps):
    count = lax.axis_size(axis)
    return lax.ppermute(value, axis, [(i, i + steps) for i in range(count - steps)])


def butterfly_sum(value, axis):
    count = lax.axis_size(axis)
    step = 1
    while step < count:
        value = value + lax.ppermute(value, axis, [(i, i ^ step) for i in range(count)])
        step *= 2
    return value


CHUNK = 64


def bias_kernel(rb_ref, cb_ref, pt_ref, g_ref, part_ref, out_ref, m_ref):
    step = pl.program_id(0)
    blocks, size, _ = m_ref.shape
    chunk = part_ref.shape[0]

    @pl.when(step == 0)
    def _():
        for a in range(blocks):
            m_ref[a] = jnp.dot(
                pt_ref[a * size:(a + 1) * size, :], g_ref[...], preferred_element_type=jnp.float32
            )

    def one(j, carry):
        t = step * chunk + j
        col = pl.multiple_of(cb_ref[t] * size, size)
        blk = m_ref[rb_ref[t], :, pl.ds(col, size)]
        prod = blk * part_ref[j, 0:size, :].astype(jnp.float32)
        out_ref[pl.ds(j, 1), :] = jnp.sum(prod, axis=0, keepdims=True)
        return carry

    lax.fori_loop(0, chunk, one, 0, unroll=2)


def tile_bias(panel_t, green, parts, rbs, cbs):
    part = parts[0]
    tiles_total, rows, size = part.shape
    orbitals = green.shape[1]
    blocks = orbitals // size
    smem = pl.BlockSpec(memory_space=pltpu.SMEM)
    return [pl.pallas_call(
        bias_kernel,
        out_shape=jax.ShapeDtypeStruct((tiles_total, size), jnp.float32),
        grid=(tiles_total // CHUNK,),
        in_specs=[
            smem,
            smem,
            pl.BlockSpec(panel_t.shape, lambda i: (0, 0)),
            pl.BlockSpec(green.shape, lambda i: (0, 0)),
            pl.BlockSpec((CHUNK, rows, size), lambda i: (i, 0, 0)),
        ],
        out_specs=pl.BlockSpec((CHUNK, size), lambda i: (i, 0)),
        scratch_shapes=[pltpu.VMEM((blocks, size, orbitals), jnp.float32)],
        compiler_params=pltpu.CompilerParams(
            dimension_semantics=("arbitrary",), vmem_limit_bytes=48 * 1024 * 1024
        ),
        interpret=INTERPRET,
    )(rbs[0], cbs[0], panel_t, green, part)]


def prop_kernel(rb_ref, cb_ref, s_ref, x_ref, part_ref, out_ref, hi_ref, lo_ref, y_ref):
    step = pl.program_id(0)
    orbitals = hi_ref.shape[0]
    size = part_ref.shape[2]
    chunk = part_ref.shape[0]

    @pl.when(step == 0)
    def _():
        hi_ref[...] = jnp.zeros(hi_ref.shape, hi_ref.dtype)
        lo_ref[...] = jnp.zeros(lo_ref.shape, lo_ref.dtype)

    def build(j, carry):
        t = step * chunk + j
        rows = pl.ds(pl.multiple_of(rb_ref[t] * size, size), size)
        cols = pl.ds(pl.multiple_of(cb_ref[t] * size, size), size)
        whole = (
            hi_ref[rows, cols].astype(jnp.float32)
            + lo_ref[rows, cols].astype(jnp.float32)
            + s_ref[t] * part_ref[j, 0:size, :].astype(jnp.float32)
        )
        upper = whole.astype(jnp.bfloat16)
        hi_ref[rows, cols] = upper
        lo_ref[rows, cols] = (whole - upper.astype(jnp.float32)).astype(jnp.bfloat16)
        return carry

    lax.fori_loop(0, chunk, build, 0)

    @pl.when(step == pl.num_programs(0) - 1)
    def _():
        span_rows = 512
        series = x_ref[...]
        running = series.astype(jnp.float32)
        for degree in range(1, TERMS + 1):
            for c in range(orbitals // span_rows):
                span = slice(c * span_rows, (c + 1) * span_rows)
                y_ref[span, :] = jnp.dot(
                    hi_ref[span, :], series, preferred_element_type=jnp.float32
                ) + jnp.dot(lo_ref[span, :], series, preferred_element_type=jnp.float32)
            series = (y_ref[...] / degree).astype(jnp.bfloat16)
            running = running + series.astype(jnp.float32)
        out_ref[...] = running.astype(out_ref.dtype)


def propagate(x0, parts, rbs, cbs, ss):
    part = parts[0]
    tiles_total, rows, size = part.shape
    orbitals, width = x0.shape
    smem = pl.BlockSpec(memory_space=pltpu.SMEM)
    return pl.pallas_call(
        prop_kernel,
        out_shape=jax.ShapeDtypeStruct((orbitals, width), jnp.bfloat16),
        grid=(tiles_total // CHUNK,),
        in_specs=[
            smem,
            smem,
            smem,
            pl.BlockSpec(x0.shape, lambda i: (0, 0)),
            pl.BlockSpec((CHUNK, rows, size), lambda i: (i, 0, 0)),
        ],
        out_specs=pl.BlockSpec((orbitals, width), lambda i: (0, 0)),
        scratch_shapes=[
            pltpu.VMEM((orbitals, orbitals), jnp.bfloat16),
            pltpu.VMEM((orbitals, orbitals), jnp.bfloat16),
            pltpu.VMEM((orbitals, width), jnp.float32),
        ],
        compiler_params=pltpu.CompilerParams(
            dimension_semantics=("arbitrary",), vmem_limit_bytes=48 * 1024 * 1024
        ),
        interpret=INTERPRET,
    )(rbs[0], cbs[0], ss[0], x0, part)


STREAMS = ((None, 0, 128),)


def xor_gather(x, order):
    for axis, step in order:
        count = lax.axis_size(axis)
        other = lax.ppermute(x, axis, [(i, i ^ step) for i in range(count)])
        x = jnp.concatenate([x, other], axis=0)
    return x


def source_tiles(order):
    position = jnp.arange(2 ** len(order), dtype=jnp.int32)
    masks = {"walker": jnp.zeros_like(position), "vec": jnp.zeros_like(position)}
    for bit, (axis, step) in enumerate(order):
        masks[axis] = masks[axis] + ((position >> bit) & 1) * step
    walker = jnp.bitwise_xor(lax.axis_index("walker"), masks["walker"])
    vec = jnp.bitwise_xor(lax.axis_index("vec"), masks["vec"])
    return walker * lax.axis_size("vec") + vec


def pick(table, index):
    hot = index[:, None] == jnp.arange(table.shape[0], dtype=index.dtype)[None, :]
    return jnp.sum(jnp.where(hot, table[None, :], jnp.zeros((), table.dtype)), axis=1)


def pad_rows(x):
    return jnp.pad(x, ((0, ROWS - x.shape[0]), (0, 0)))


def shards(
    copy_counts, panels, inverse_intersection, trial_orbitals, chol_tiles, tile_blocks, aux_fields
):
    cols_local = panels.shape[1]
    walker_id = lax.axis_index("walker")
    vecs = lax.axis_size("vec")
    prev_panel = shift_from(panels, "walker", 1)
    prev_inverse = shift_from(inverse_intersection, "walker", 1)
    size = chol_tiles.shape[2]
    meta = jnp.zeros((1, 16, size), chol_tiles.dtype).at[0, 0, 0].set(copy_counts[0].astype(chol_tiles.dtype))
    payload = jnp.concatenate([chol_tiles, meta], axis=1)
    order = (("vec", 4), ("vec", 2), ("vec", 1))
    gathered = lax.all_gather(xor_gather(payload, order), "walker", axis=0, tiled=True)
    tiles_rows = chol_tiles.shape[1]
    counts = gathered[::vecs, tiles_rows, 0].astype(jnp.float32)
    walkers = jnp.arange(counts.shape[0])
    surplus = jnp.sum(jnp.where(walkers < walker_id, counts, 0.0)) - walker_id.astype(jnp.float32)
    from_prev = surplus > 0.5
    local = source_tiles(order) % vecs
    source = (walkers[:, None] * vecs + local[None, :]).reshape(-1)
    rbs = [pick(tile_blocks[:, 0], source)]
    cbs = [pick(tile_blocks[:, 1], source)]
    parts = [gathered]

    green_own = jnp.dot(inverse_intersection[0], trial_orbitals, preferred_element_type=jnp.float32).astype(jnp.bfloat16)
    green_prev = jnp.dot(prev_inverse[0], trial_orbitals, preferred_element_type=jnp.float32).astype(jnp.bfloat16)
    start = jnp.where(from_prev, prev_panel[0], panels[0])
    green = jnp.where(from_prev, green_prev, green_own)
    partials = tile_bias(pad_rows(start).T, pad_rows(green), parts, rbs, cbs)
    vectors = tile_blocks.shape[0] // KT
    values = partials[0].sum(axis=1)
    hot = (source // KT)[:, None] == jnp.arange(vectors, dtype=source.dtype)[None, :]
    per_vector = jnp.sum(jnp.where(hot, values[:, None], 0.0), axis=0)
    raw = butterfly_sum(per_vector, "vec")
    bias = jnp.clip(TIME_STEP_ROOT * raw, -1.0, 1.0)
    scales = TIME_STEP_ROOT * (aux_fields[0] - bias)
    ss = [pick(scales, source // KT)]
    out = propagate(pad_rows(start).T, parts, rbs, cbs, ss)
    return out.T[:cols_local][None]


def solution(mesh):
    return jax.shard_map(
        shards,
        mesh=mesh,
        in_specs=(
            P("walker"),
            P("walker", "vec", None),
            P("walker", "vec", None),
            P(),
            P(("walker", "vec"), None, None),
            P(),
            P("walker", None),
        ),
        out_specs=P("walker", "vec", None),
        check_vma=False,
    )
```

```python
import functools

import jax
import jax.numpy as jnp
from jax import lax
from jax.experimental import pallas as pl
from jax.experimental.pallas import tpu as pltpu
from jax.sharding import PartitionSpec as P

KT = 4
TERMS = 3
TIME_STEP_ROOT = 0.1
ROWS = 32
INTERPRET = False


def shift_from(value, axis, steps):
    count = lax.axis_size(axis)
    return lax.ppermute(value, axis, [(i, i + steps) for i in range(count - steps)])


def butterfly_sum(value, axis):
    count = lax.axis_size(axis)
    step = 1
    while step < count:
        value = value + lax.ppermute(value, axis, [(i, i ^ step) for i in range(count)])
        step *= 2
    return value


CHUNK = 128


def bias_kernel(rb_ref, cb_ref, pt_ref, g_ref, part_ref, out_ref, m_ref):
    step = pl.program_id(0)
    blocks, size, _ = m_ref.shape
    chunk = part_ref.shape[0]

    @pl.when(step == 0)
    def _():
        for a in range(blocks):
            m_ref[a] = jnp.dot(
                pt_ref[a * size:(a + 1) * size, :], g_ref[...], preferred_element_type=jnp.float32
            )

    def one(j, carry):
        t = step * chunk + j
        col = pl.multiple_of(cb_ref[t] * size, size)
        blk = m_ref[rb_ref[t], :, pl.ds(col, size)]
        prod = blk * part_ref[j, 0:size, :].astype(jnp.float32)
        out_ref[pl.ds(j, 1), :] = jnp.sum(prod, axis=0, keepdims=True)
        return carry

    lax.fori_loop(0, chunk, one, 0, unroll=2)


def tile_bias(panel_t, green, parts, rbs, cbs):
    part = parts[0]
    tiles_total, rows, size = part.shape
    orbitals = green.shape[1]
    blocks = orbitals // size
    smem = pl.BlockSpec(memory_space=pltpu.SMEM)
    return [pl.pallas_call(
        bias_kernel,
        out_shape=jax.ShapeDtypeStruct((tiles_total, size), jnp.float32),
        grid=(tiles_total // CHUNK,),
        in_specs=[
            smem,
            smem,
            pl.BlockSpec(panel_t.shape, lambda i: (0, 0)),
            pl.BlockSpec(green.shape, lambda i: (0, 0)),
            pl.BlockSpec((CHUNK, rows, size), lambda i: (i, 0, 0)),
        ],
        out_specs=pl.BlockSpec((CHUNK, size), lambda i: (i, 0)),
        scratch_shapes=[pltpu.VMEM((blocks, size, orbitals), jnp.float32)],
        compiler_params=pltpu.CompilerParams(
            dimension_semantics=("arbitrary",), vmem_limit_bytes=48 * 1024 * 1024
        ),
        interpret=INTERPRET,
    )(rbs[0], cbs[0], panel_t, green, part)]


def prop_kernel(rb_ref, cb_ref, s_ref, x_ref, part_ref, out_ref, hi_ref, lo_ref, y_ref):
    step = pl.program_id(0)
    orbitals = hi_ref.shape[0]
    size = part_ref.shape[2]
    chunk = part_ref.shape[0]

    @pl.when(step == 0)
    def _():
        hi_ref[...] = jnp.zeros(hi_ref.shape, hi_ref.dtype)
        lo_ref[...] = jnp.zeros(lo_ref.shape, lo_ref.dtype)

    def build(j, carry):
        t = step * chunk + j
        rows = pl.ds(pl.multiple_of(rb_ref[t] * size, size), size)
        cols = pl.ds(pl.multiple_of(cb_ref[t] * size, size), size)
        whole = (
            hi_ref[rows, cols].astype(jnp.float32)
            + lo_ref[rows, cols].astype(jnp.float32)
            + s_ref[t] * part_ref[j, 0:size, :].astype(jnp.float32)
        )
        upper = whole.astype(jnp.bfloat16)
        hi_ref[rows, cols] = upper
        lo_ref[rows, cols] = (whole - upper.astype(jnp.float32)).astype(jnp.bfloat16)
        return carry

    lax.fori_loop(0, chunk, build, 0)

    @pl.when(step == pl.num_programs(0) - 1)
    def _():
        span_rows = 512
        series = x_ref[...]
        running = series.astype(jnp.float32)
        for degree in range(1, TERMS + 1):
            for c in range(orbitals // span_rows):
                span = slice(c * span_rows, (c + 1) * span_rows)
                y_ref[span, :] = jnp.dot(
                    hi_ref[span, :], series, preferred_element_type=jnp.float32
                ) + jnp.dot(lo_ref[span, :], series, preferred_element_type=jnp.float32)
            series = (y_ref[...] / degree).astype(jnp.bfloat16)
            running = running + series.astype(jnp.float32)
        out_ref[...] = running.astype(out_ref.dtype)


def propagate(x0, parts, rbs, cbs, ss):
    part = parts[0]
    tiles_total, rows, size = part.shape
    orbitals, width = x0.shape
    smem = pl.BlockSpec(memory_space=pltpu.SMEM)
    return pl.pallas_call(
        prop_kernel,
        out_shape=jax.ShapeDtypeStruct((orbitals, width), jnp.bfloat16),
        grid=(tiles_total // CHUNK,),
        in_specs=[
            smem,
            smem,
            smem,
            pl.BlockSpec(x0.shape, lambda i: (0, 0)),
            pl.BlockSpec((CHUNK, rows, size), lambda i: (i, 0, 0)),
        ],
        out_specs=pl.BlockSpec((orbitals, width), lambda i: (0, 0)),
        scratch_shapes=[
            pltpu.VMEM((orbitals, orbitals), jnp.bfloat16),
            pltpu.VMEM((orbitals, orbitals), jnp.bfloat16),
            pltpu.VMEM((orbitals, width), jnp.float32),
        ],
        compiler_params=pltpu.CompilerParams(
            dimension_semantics=("arbitrary",), vmem_limit_bytes=48 * 1024 * 1024
        ),
        interpret=INTERPRET,
    )(rbs[0], cbs[0], ss[0], x0, part)


STREAMS = ((None, 0, 128),)


def xor_gather(x, order):
    for axis, step in order:
        count = lax.axis_size(axis)
        other = lax.ppermute(x, axis, [(i, i ^ step) for i in range(count)])
        x = jnp.concatenate([x, other], axis=0)
    return x


def source_tiles(order):
    position = jnp.arange(2 ** len(order), dtype=jnp.int32)
    masks = {"walker": jnp.zeros_like(position), "vec": jnp.zeros_like(position)}
    for bit, (axis, step) in enumerate(order):
        masks[axis] = masks[axis] + ((position >> bit) & 1) * step
    walker = jnp.bitwise_xor(lax.axis_index("walker"), masks["walker"])
    vec = jnp.bitwise_xor(lax.axis_index("vec"), masks["vec"])
    return walker * lax.axis_size("vec") + vec


def pick(table, index):
    hot = index[:, None] == jnp.arange(table.shape[0], dtype=index.dtype)[None, :]
    return jnp.sum(jnp.where(hot, table[None, :], jnp.zeros((), table.dtype)), axis=1)


def pad_rows(x):
    return jnp.pad(x, ((0, ROWS - x.shape[0]), (0, 0)))


def shards(
    copy_counts, panels, inverse_intersection, trial_orbitals, chol_tiles, tile_blocks, aux_fields
):
    cols_local = panels.shape[1]
    walker_id = lax.axis_index("walker")
    vecs = lax.axis_size("vec")
    prev_panel = shift_from(panels, "walker", 1)
    prev_inverse = shift_from(inverse_intersection, "walker", 1)
    size = chol_tiles.shape[2]
    meta = jnp.zeros((1, 16, size), chol_tiles.dtype).at[0, 0, 0].set(copy_counts[0].astype(chol_tiles.dtype))
    payload = jnp.concatenate([chol_tiles, meta], axis=1)
    order = (("vec", 4), ("vec", 2), ("vec", 1))
    gathered = lax.all_gather(xor_gather(payload, order), "walker", axis=0, tiled=True)
    tiles_rows = chol_tiles.shape[1]
    counts = gathered[::vecs, tiles_rows, 0].astype(jnp.float32)
    walkers = jnp.arange(counts.shape[0])
    surplus = jnp.sum(jnp.where(walkers < walker_id, counts, 0.0)) - walker_id.astype(jnp.float32)
    from_prev = surplus > 0.5
    local = source_tiles(order) % vecs
    source = (walkers[:, None] * vecs + local[None, :]).reshape(-1)
    rbs = [pick(tile_blocks[:, 0], source)]
    cbs = [pick(tile_blocks[:, 1], source)]
    parts = [gathered]

    green_own = jnp.dot(inverse_intersection[0], trial_orbitals, preferred_element_type=jnp.float32).astype(jnp.bfloat16)
    green_prev = jnp.dot(prev_inverse[0], trial_orbitals, preferred_element_type=jnp.float32).astype(jnp.bfloat16)
    start = jnp.where(from_prev, prev_panel[0], panels[0])
    green = jnp.where(from_prev, green_prev, green_own)
    partials = tile_bias(pad_rows(start).T, pad_rows(green), parts, rbs, cbs)
    vectors = tile_blocks.shape[0] // KT
    values = partials[0].sum(axis=1)
    hot = (source // KT)[:, None] == jnp.arange(vectors, dtype=source.dtype)[None, :]
    per_vector = jnp.sum(jnp.where(hot, values[:, None], 0.0), axis=0)
    raw = butterfly_sum(per_vector, "vec")
    bias = jnp.clip(TIME_STEP_ROOT * raw, -1.0, 1.0)
    scales = TIME_STEP_ROOT * (aux_fields[0] - bias)
    ss = [pick(scales, source // KT)]
    out = propagate(pad_rows(start).T, parts, rbs, cbs, ss)
    return out.T[:cols_local][None]


def solution(mesh):
    return jax.shard_map(
        shards,
        mesh=mesh,
        in_specs=(
            P("walker"),
            P("walker", "vec", None),
            P("walker", "vec", None),
            P(),
            P(("walker", "vec"), None, None),
            P(),
            P("walker", None),
        ),
        out_specs=P("walker", "vec", None),
        check_vma=False,
    )
```

```python
import functools

import jax
import jax.numpy as jnp
from jax import lax
from jax.experimental import pallas as pl
from jax.experimental.pallas import tpu as pltpu
from jax.sharding import PartitionSpec as P

KT = 4
TERMS = 3
TIME_STEP_ROOT = 0.1
ROWS = 32
INTERPRET = False


def shift_from(value, axis, steps):
    count = lax.axis_size(axis)
    return lax.ppermute(value, axis, [(i, i + steps) for i in range(count - steps)])


def butterfly_sum(value, axis):
    count = lax.axis_size(axis)
    step = 1
    while step < count:
        value = value + lax.ppermute(value, axis, [(i, i ^ step) for i in range(count)])
        step *= 2
    return value


CHUNK = 64


def bias_kernel(rb_ref, cb_ref, pt_ref, g_ref, part_ref, out_ref, m_ref):
    step = pl.program_id(0)
    blocks, size, _ = m_ref.shape
    chunk = part_ref.shape[0]

    @pl.when(step == 0)
    def _():
        for a in range(blocks):
            m_ref[a] = jnp.dot(
                pt_ref[a * size:(a + 1) * size, :], g_ref[...], preferred_element_type=jnp.float32
            )

    def one(j, carry):
        t = step * chunk + j
        col = pl.multiple_of(cb_ref[t] * size, size)
        blk = m_ref[rb_ref[t], :, pl.ds(col, size)]
        prod = blk * part_ref[j, 0:size, :].astype(jnp.float32)
        out_ref[pl.ds(j, 1), :] = jnp.sum(prod, axis=0, keepdims=True)
        return carry

    lax.fori_loop(0, chunk, one, 0, unroll=4)


def tile_bias(panel_t, green, parts, rbs, cbs):
    part = parts[0]
    tiles_total, rows, size = part.shape
    orbitals = green.shape[1]
    blocks = orbitals // size
    smem = pl.BlockSpec(memory_space=pltpu.SMEM)
    return [pl.pallas_call(
        bias_kernel,
        out_shape=jax.ShapeDtypeStruct((tiles_total, size), jnp.float32),
        grid=(tiles_total // CHUNK,),
        in_specs=[
            smem,
            smem,
            pl.BlockSpec(panel_t.shape, lambda i: (0, 0)),
            pl.BlockSpec(green.shape, lambda i: (0, 0)),
            pl.BlockSpec((CHUNK, rows, size), lambda i: (i, 0, 0)),
        ],
        out_specs=pl.BlockSpec((CHUNK, size), lambda i: (i, 0)),
        scratch_shapes=[pltpu.VMEM((blocks, size, orbitals), jnp.float32)],
        compiler_params=pltpu.CompilerParams(
            dimension_semantics=("arbitrary",), vmem_limit_bytes=48 * 1024 * 1024
        ),
        interpret=INTERPRET,
    )(rbs[0], cbs[0], panel_t, green, part)]


def prop_kernel(rb_ref, cb_ref, s_ref, x_ref, part_ref, out_ref, hi_ref, lo_ref, y_ref):
    step = pl.program_id(0)
    orbitals = hi_ref.shape[0]
    size = part_ref.shape[2]
    chunk = part_ref.shape[0]

    @pl.when(step == 0)
    def _():
        hi_ref[...] = jnp.zeros(hi_ref.shape, hi_ref.dtype)
        lo_ref[...] = jnp.zeros(lo_ref.shape, lo_ref.dtype)

    def build(j, carry):
        t = step * chunk + j
        rows = pl.ds(pl.multiple_of(rb_ref[t] * size, size), size)
        cols = pl.ds(pl.multiple_of(cb_ref[t] * size, size), size)
        whole = (
            hi_ref[rows, cols].astype(jnp.float32)
            + lo_ref[rows, cols].astype(jnp.float32)
            + s_ref[t] * part_ref[j, 0:size, :].astype(jnp.float32)
        )
        upper = whole.astype(jnp.bfloat16)
        hi_ref[rows, cols] = upper
        lo_ref[rows, cols] = (whole - upper.astype(jnp.float32)).astype(jnp.bfloat16)
        return carry

    lax.fori_loop(0, chunk, build, 0)

    @pl.when(step == pl.num_programs(0) - 1)
    def _():
        span_rows = 512
        series = x_ref[...]
        running = series.astype(jnp.float32)
        for degree in range(1, TERMS + 1):
            for c in range(orbitals // span_rows):
                span = slice(c * span_rows, (c + 1) * span_rows)
                y_ref[span, :] = jnp.dot(
                    hi_ref[span, :], series, preferred_element_type=jnp.float32
                ) + jnp.dot(lo_ref[span, :], series, preferred_element_type=jnp.float32)
            series = (y_ref[...] / degree).astype(jnp.bfloat16)
            running = running + series.astype(jnp.float32)
        out_ref[...] = running.astype(out_ref.dtype)


def propagate(x0, parts, rbs, cbs, ss):
    part = parts[0]
    tiles_total, rows, size = part.shape
    orbitals, width = x0.shape
    smem = pl.BlockSpec(memory_space=pltpu.SMEM)
    return pl.pallas_call(
        prop_kernel,
        out_shape=jax.ShapeDtypeStruct((orbitals, width), jnp.bfloat16),
        grid=(tiles_total // CHUNK,),
        in_specs=[
            smem,
            smem,
            smem,
            pl.BlockSpec(x0.shape, lambda i: (0, 0)),
            pl.BlockSpec((CHUNK, rows, size), lambda i: (i, 0, 0)),
        ],
        out_specs=pl.BlockSpec((orbitals, width), lambda i: (0, 0)),
        scratch_shapes=[
            pltpu.VMEM((orbitals, orbitals), jnp.bfloat16),
            pltpu.VMEM((orbitals, orbitals), jnp.bfloat16),
            pltpu.VMEM((orbitals, width), jnp.float32),
        ],
        compiler_params=pltpu.CompilerParams(
            dimension_semantics=("arbitrary",), vmem_limit_bytes=48 * 1024 * 1024
        ),
        interpret=INTERPRET,
    )(rbs[0], cbs[0], ss[0], x0, part)


STREAMS = ((None, 0, 128),)


def xor_gather(x, order):
    for axis, step in order:
        count = lax.axis_size(axis)
        other = lax.ppermute(x, axis, [(i, i ^ step) for i in range(count)])
        x = jnp.concatenate([x, other], axis=0)
    return x


def source_tiles(order):
    position = jnp.arange(2 ** len(order), dtype=jnp.int32)
    masks = {"walker": jnp.zeros_like(position), "vec": jnp.zeros_like(position)}
    for bit, (axis, step) in enumerate(order):
        masks[axis] = masks[axis] + ((position >> bit) & 1) * step
    walker = jnp.bitwise_xor(lax.axis_index("walker"), masks["walker"])
    vec = jnp.bitwise_xor(lax.axis_index("vec"), masks["vec"])
    return walker * lax.axis_size("vec") + vec


def pick(table, index):
    hot = index[:, None] == jnp.arange(table.shape[0], dtype=index.dtype)[None, :]
    return jnp.sum(jnp.where(hot, table[None, :], jnp.zeros((), table.dtype)), axis=1)


def pad_rows(x):
    return jnp.pad(x, ((0, ROWS - x.shape[0]), (0, 0)))


def shards(
    copy_counts, panels, inverse_intersection, trial_orbitals, chol_tiles, tile_blocks, aux_fields
):
    cols_local = panels.shape[1]
    walker_id = lax.axis_index("walker")
    vecs = lax.axis_size("vec")
    prev_panel = shift_from(panels, "walker", 1)
    prev_inverse = shift_from(inverse_intersection, "walker", 1)
    size = chol_tiles.shape[2]
    meta = jnp.zeros((1, 16, size), chol_tiles.dtype).at[0, 0, 0].set(copy_counts[0].astype(chol_tiles.dtype))
    payload = jnp.concatenate([chol_tiles, meta], axis=1)
    order = (("vec", 4), ("vec", 2), ("vec", 1))
    gathered = lax.all_gather(xor_gather(payload, order), "walker", axis=0, tiled=True)
    tiles_rows = chol_tiles.shape[1]
    counts = gathered[::vecs, tiles_rows, 0].astype(jnp.float32)
    walkers = jnp.arange(counts.shape[0])
    surplus = jnp.sum(jnp.where(walkers < walker_id, counts, 0.0)) - walker_id.astype(jnp.float32)
    from_prev = surplus > 0.5
    local = source_tiles(order) % vecs
    source = (walkers[:, None] * vecs + local[None, :]).reshape(-1)
    rbs = [pick(tile_blocks[:, 0], source)]
    cbs = [pick(tile_blocks[:, 1], source)]
    parts = [gathered]

    green_own = jnp.dot(inverse_intersection[0], trial_orbitals, preferred_element_type=jnp.float32).astype(jnp.bfloat16)
    green_prev = jnp.dot(prev_inverse[0], trial_orbitals, preferred_element_type=jnp.float32).astype(jnp.bfloat16)
    start = jnp.where(from_prev, prev_panel[0], panels[0])
    green = jnp.where(from_prev, green_prev, green_own)
    partials = tile_bias(pad_rows(start).T, pad_rows(green), parts, rbs, cbs)
    vectors = tile_blocks.shape[0] // KT
    values = partials[0].sum(axis=1)
    hot = (source // KT)[:, None] == jnp.arange(vectors, dtype=source.dtype)[None, :]
    per_vector = jnp.sum(jnp.where(hot, values[:, None], 0.0), axis=0)
    raw = butterfly_sum(per_vector, "vec")
    bias = jnp.clip(TIME_STEP_ROOT * raw, -1.0, 1.0)
    scales = TIME_STEP_ROOT * (aux_fields[0] - bias)
    ss = [pick(scales, source // KT)]
    out = propagate(pad_rows(start).T, parts, rbs, cbs, ss)
    return out.T[:cols_local][None]


def solution(mesh):
    return jax.shard_map(
        shards,
        mesh=mesh,
        in_specs=(
            P("walker"),
            P("walker", "vec", None),
            P("walker", "vec", None),
            P(),
            P(("walker", "vec"), None, None),
            P(),
            P("walker", None),
        ),
        out_specs=P("walker", "vec", None),
        check_vma=False,
    )
```
